128 devices in a mesh: ctx: 8 (over x, y_hi), head: 16 (over y_lo, z, core).
Axes of the slice: x: 4, y: 4 (y_hi: 2, y_lo: 2; y = y_hi * 2 + y_lo), z: 4, core: 2. Of those that a mesh axis runs over, the one named last changes fastest.
Arguments:
- hidden_in: bfloat16 [8192, 5376], P(('ctx', 'head')), may hold values from -6 to 6
- pre_gain: float32 [5376], replicated, may hold values from 0.1 to 1.9
- w_query: bfloat16 [5376, 4096], P('ctx', 'head'), may hold values from -0.054554473 to 0.054554473, as said below
- w_key: bfloat16 [5376, 2048], P('ctx', 'head'), may hold values from -0.054554473 to 0.054554473, as said below
- value_weight: bfloat16 [5376, 2048], P('ctx', 'head'), may hold values from -0.078125 to 0.078125
- query_gain: float32 [128], replicated, may hold values from 0.6 to 7, as said below
- key_norm_gain: float32 [128], replicated, may hold values from 0.6 to 7, as said below
- w_output: bfloat16 [4096, 5376], P(('head', 'ctx')), may hold values from -0.09375 to 0.09375
- post_gain: float32 [5376], replicated, may hold values from 0.1 to 1.9
Outputs:
- layer_out: bfloat16 [8192, 5376], P(('ctx', 'head'))
The draws below stay inside these ranges and needn't reach their ends.
Inputs may be any that keep to these rules, and one draw needn't show every extreme that they name: `w_query`: entries are normal draws clipped to 4 standard deviations, scaled by 5376 ** -0.5. `w_key`: entries are normal draws clipped to 4 standard deviations, scaled by 5376 ** -0.5. `query_gain`: positive gains. `key_norm_gain`: positive gains.
All inputs are finite; a program needn't handle non-finite values.
Results may differ from the reference program's by a relative error of at most 0.015.
The reference program's roundings to bfloat16 on the way count: a program that leaves them out, or rounds other values in their place, can miss the bound.
Values may be sent and summed in bfloat16 or wider, within the bound.
No kernel may reach another device: no remote copies, remote signals or barrier semaphores. Data moves between devices by JAX's collectives and lax.ppermute only.
A program may use at most 64 MiB of HBM per device.

```python
import jax
import jax.numpy as jnp
from jax import lax

MODEL_WIDTH = 5376
QUERY_HEADS = 32
KEY_VALUE_HEADS = 16
HEAD_SIZE = 128
WINDOW_SPAN = 1024
TOK_DEV = 1024
SLAB_TOKENS = 8192
N_HEAD = 16


def common_query(key):
    fresh_sample = jax.random.normal(jax.random.fold_in(key, 7), (MODEL_WIDTH, QUERY_HEADS * HEAD_SIZE), jnp.float32)
    return jnp.clip(fresh_sample, -4.0, 4.0) * MODEL_WIDTH ** (-0.5)


def draw_w_query(key, part):
    return common_query(key).astype(jnp.bfloat16)


def draw_w_key(key, part):
    fresh_sample = jax.random.normal(jax.random.fold_in(key, 8), (MODEL_WIDTH, KEY_VALUE_HEADS * HEAD_SIZE), jnp.float32)
    parent_sample = jnp.clip(fresh_sample, -4.0, 4.0) * MODEL_WIDTH ** (-0.5)
    return parent_sample.astype(jnp.bfloat16)


def gain_draw(key, salt):
    uniform_draw = jax.random.uniform(jax.random.fold_in(key, salt), (HEAD_SIZE,), jnp.float32)
    lower_end = jnp.log(0.6)
    upper_end = jnp.log(1.6)
    return jnp.exp(lower_end + uniform_draw * (upper_end - lower_end))


def draw_query_gain(key, part):
    return gain_draw(key, 21)


def draw_key_norm_gain(key, part):
    return gain_draw(key, 22)


def shard_levels(key, extent, shards, least, high):
    gain = 1.0
    for axis_at, shards_of in shards:
        draws = jax.random.uniform(jax.random.fold_in(jax.random.fold_in(key, 6), axis_at), (shards_of,), jnp.float32, least / len(shards), high / len(shards))
        gain = gain * jnp.repeat(jnp.exp(draws), extent[axis_at] // shards_of).reshape((-1,) + (1,) * (len(extent) - 1 - axis_at))
    return gain


def scatter_about(key, dims, spread, bound, split=(), kind=jnp.bfloat16):
    array = spread * jax.random.normal(key, dims, jnp.float32)
    if split:
        array = array * shard_levels(key, dims, split, -0.22, 0.18)
    return jnp.clip(array, -bound, bound).astype(kind)


def setup_inputs(seed: int = 0) -> dict:
    streams_of = jax.random.split(jax.random.key(seed), 10)
    hidden_in = scatter_about(streams_of[0], (SLAB_TOKENS, MODEL_WIDTH), 1.0, 6.0, ((0, 128),))
    pre_gain = jnp.clip(1.0 + 0.18 * jax.random.normal(streams_of[1], (MODEL_WIDTH,), jnp.float32), 0.1, 1.9)
    w_query = draw_w_query(jax.random.fold_in(streams_of[9], 71), 0)
    w_key = draw_w_key(jax.random.fold_in(streams_of[9], 71), 0)
    value_weight = scatter_about(streams_of[4], (MODEL_WIDTH, KEY_VALUE_HEADS * HEAD_SIZE), MODEL_WIDTH ** -0.5, 0.078125, ((0, 8), (1, 16)))
    query_gain = draw_query_gain(jax.random.fold_in(streams_of[9], 71), 0)
    key_norm_gain = draw_key_norm_gain(jax.random.fold_in(streams_of[9], 71), 0)
    w_output = scatter_about(streams_of[7], (QUERY_HEADS * HEAD_SIZE, MODEL_WIDTH), (QUERY_HEADS * HEAD_SIZE) ** -0.5, 0.09375, ((0, 128),))
    post_gain = jnp.clip(1.0 + 0.18 * jax.random.normal(streams_of[8], (MODEL_WIDTH,), jnp.float32), 0.1, 1.9)
    return dict(hidden_in=hidden_in, pre_gain=pre_gain, w_query=w_query, w_key=w_key, value_weight=value_weight, query_gain=query_gain, key_norm_gain=key_norm_gain, w_output=w_output, post_gain=post_gain)


norm_eps = 1e-06
query_scale = 168.0 ** (-0.5)
rope_base = 10000.0
mask_value = -1e+30

def root_mean_scale(values, scaling):
    mean_sq = lax.optimization_barrier(jnp.mean(values * values, axis=-1, keepdims=True))
    return values * lax.rsqrt(mean_sq + norm_eps) * scaling

def apply_rotary(values, token_places):
    full_width = values.shape[-1]
    half_width = full_width // 2
    frequency = rope_base ** (-jnp.arange(half_width, dtype=jnp.float32) * 2.0 / full_width)
    angles = token_places.astype(jnp.float32)[:, None] * frequency[None, :]
    cosine = jnp.cos(angles)[:, None, :]
    sine_part = jnp.sin(angles)[:, None, :]
    lower_half = values[..., :half_width]
    upper_half = values[..., half_width:]
    return jnp.concatenate([lower_half * cosine - upper_half * sine_part, upper_half * cosine + lower_half * sine_part], axis=-1)

def reference(hidden_in, pre_gain, w_query, w_key, value_weight, query_gain, key_norm_gain, w_output, post_gain):
    own_rows = hidden_in.astype(jnp.float32)
    normed = root_mean_scale(own_rows, pre_gain.astype(jnp.float32)).astype(jnp.bfloat16)
    query_raw = jnp.dot(normed, w_query, preferred_element_type=jnp.float32)
    key_unnormed = jnp.dot(normed, w_key, preferred_element_type=jnp.float32)
    value_unnormed = jnp.dot(normed, value_weight, preferred_element_type=jnp.float32)
    token_places = jnp.arange(SLAB_TOKENS, dtype=jnp.int32)
    query_matrix = (apply_rotary(root_mean_scale(query_raw.reshape(SLAB_TOKENS, QUERY_HEADS, HEAD_SIZE), query_gain.astype(jnp.float32)), token_places) * query_scale).astype(jnp.bfloat16)
    projected_keys = apply_rotary(root_mean_scale(key_unnormed.reshape(SLAB_TOKENS, KEY_VALUE_HEADS, HEAD_SIZE), key_norm_gain.astype(jnp.float32)), token_places).astype(jnp.bfloat16)
    projected_values = value_unnormed.astype(jnp.bfloat16).reshape(SLAB_TOKENS, KEY_VALUE_HEADS, HEAD_SIZE)
    heads_per_group = QUERY_HEADS // KEY_VALUE_HEADS
    block_rows = min(512, TOK_DEV)
    leading_zeros = jnp.zeros((WINDOW_SPAN, KEY_VALUE_HEADS, HEAD_SIZE), jnp.bfloat16)
    padded_keys = jnp.concatenate([leading_zeros, projected_keys], axis=0)
    padded_values = jnp.concatenate([leading_zeros, projected_values], axis=0)
    grouped_queries = query_matrix.reshape(SLAB_TOKENS, KEY_VALUE_HEADS, heads_per_group, HEAD_SIZE)

    def one_block(block_index):
        first_row = block_index * block_rows
        query_block = lax.dynamic_slice_in_dim(grouped_queries, first_row, block_rows, 0)
        key_block = lax.dynamic_slice_in_dim(padded_keys, first_row, block_rows + WINDOW_SPAN, 0)
        value_block = lax.dynamic_slice_in_dim(padded_values, first_row, block_rows + WINDOW_SPAN, 0)
        scores = jnp.einsum('qjgd,kjd->jgqk', query_block.astype(jnp.float32), key_block.astype(jnp.float32))
        query_spots = first_row + jnp.arange(block_rows, dtype=jnp.int32)
        key_spots = first_row - WINDOW_SPAN + jnp.arange(block_rows + WINDOW_SPAN, dtype=jnp.int32)
        allowed = (key_spots[None, :] <= query_spots[:, None]) & (key_spots[None, :] > query_spots[:, None] - WINDOW_SPAN) & (key_spots[None, :] >= 0)
        scores = jnp.where(allowed, scores, mask_value)
        row_max = lax.optimization_barrier(jnp.max(scores, axis=-1, keepdims=True))
        weights = jnp.exp(scores - row_max)
        row_sum = lax.optimization_barrier(jnp.sum(weights, axis=-1, keepdims=True))
        probabilities = (weights / row_sum).astype(jnp.bfloat16)
        mixed = jnp.einsum('jgqk,kjd->qjgd', probabilities.astype(jnp.float32), value_block.astype(jnp.float32))
        return mixed.astype(jnp.bfloat16).reshape(block_rows, QUERY_HEADS * HEAD_SIZE)
    attended = lax.map(one_block, jnp.arange(SLAB_TOKENS // block_rows, dtype=jnp.int32)).reshape(SLAB_TOKENS, QUERY_HEADS * HEAD_SIZE)
    group_width = QUERY_HEADS * HEAD_SIZE // N_HEAD

    def add_group(carried, group_index):
        columns = lax.dynamic_slice_in_dim(attended, group_index * group_width, group_width, 1)
        weight_rows = lax.dynamic_slice_in_dim(w_output, group_index * group_width, group_width, 0)
        partial_value = jnp.dot(columns, weight_rows, preferred_element_type=jnp.float32).astype(jnp.bfloat16)
        partial_value = lax.optimization_barrier(partial_value).astype(jnp.float32)
        return (carried + partial_value, None)
    summed, unused = lax.scan(add_group, jnp.zeros((SLAB_TOKENS, MODEL_WIDTH), jnp.float32), jnp.arange(N_HEAD, dtype=jnp.int32))
    return (own_rows + root_mean_scale(summed, post_gain.astype(jnp.float32))).astype(jnp.bfloat16)
```

```python
import jax
import jax.numpy as jnp
from jax import lax
from jax.sharding import Mesh, PartitionSpec as P

HEAD_SIZE = 128
WINDOW_SPAN = 1024


norm_eps = 1e-06
query_scale = 168.0 ** (-0.5)
rope_base = 10000.0
mask_value = -1e30


def passed_along(shard, axis, by):
    count = lax.axis_size(axis)
    pairs = [(i, i + by) for i in range(count) if 0 <= i + by < count]
    return lax.ppermute(shard, axis, pairs)


def rotated(shard, axis, by):
    count = lax.axis_size(axis)
    pairs = [(i, (i + by) % count) for i in range(count)]
    return lax.ppermute(shard, axis, pairs)


def gathered_by_permutes(shard, axis):
    count = lax.axis_size(axis)
    me = lax.axis_index(axis)
    stacked = jnp.zeros((count,) + shard.shape, shard.dtype)
    stacked = lax.dynamic_update_index_in_dim(stacked, shard, me, 0)
    for by in range(1, count):
        piece = rotated(shard, axis, by)
        stacked = lax.dynamic_update_index_in_dim(stacked, piece, (me - by) % count, 0)
    return stacked.reshape((count * shard.shape[0],) + shard.shape[1:])


def root_mean_scale(values, scaling):
    mean_sq = jnp.mean(values * values, axis=-1, keepdims=True)
    return values * lax.rsqrt(mean_sq + norm_eps) * scaling


def apply_rotary(values, token_places):
    full_width = values.shape[-1]
    half_width = full_width // 2
    frequency = rope_base ** (-jnp.arange(half_width, dtype=jnp.float32) * 2.0 / full_width)
    angles = token_places.astype(jnp.float32)[:, None] * frequency[None, :]
    cosine = jnp.cos(angles)[:, None, :]
    sine_part = jnp.sin(angles)[:, None, :]
    lower_half = values[..., :half_width]
    upper_half = values[..., half_width:]
    return jnp.concatenate(
        [
            lower_half * cosine - upper_half * sine_part,
            upper_half * cosine + lower_half * sine_part,
        ],
        axis=-1,
    )


def interleave(mine, other, core, chips, rows):
    first = jnp.where(core == 0, mine, other)
    second = jnp.where(core == 0, other, mine)
    width = mine.shape[-1]
    return jnp.stack(
        [first.reshape(chips, rows, width), second.reshape(chips, rows, width)], axis=1
    ).reshape(chips * 2 * rows, width)


def body(
    hidden_in,
    pre_gain,
    w_query,
    w_key,
    value_weight,
    query_gain,
    key_norm_gain,
    w_output,
    post_gain,
):
    core = lax.axis_index("core")
    chips = lax.axis_size("hc")
    rows = hidden_in.shape[0]
    own_rows = hidden_in.astype(jnp.float32)

    q_cols = w_query.shape[1]
    k_cols = w_key.shape[1]
    w_in = gathered_by_permutes(jnp.concatenate([w_query, w_key, value_weight], axis=1), "ctx")
    out_weight = gathered_by_permutes(w_output, "ctx")

    mine_rows = lax.all_gather(hidden_in, "hc", axis=0, tiled=True)
    other_rows = rotated(mine_rows, "core", 1)

    def project(raw):
        normed = root_mean_scale(raw.astype(jnp.float32), pre_gain).astype(jnp.bfloat16)
        return jnp.dot(normed, w_in, preferred_element_type=jnp.float32)

    projected = interleave(project(mine_rows), project(other_rows), core, chips, rows)
    tok_count = projected.shape[0]
    query_raw = projected[:, :q_cols]
    key_unnormed = projected[:, q_cols : q_cols + k_cols]
    value_unnormed = projected[:, q_cols + k_cols :]

    local_heads = q_cols // HEAD_SIZE
    local_groups = k_cols // HEAD_SIZE
    heads_per_group = local_heads // local_groups
    ctx_index = lax.axis_index("ctx")
    token_places = ctx_index * tok_count + jnp.arange(tok_count, dtype=jnp.int32)
    query_matrix = (
        apply_rotary(
            root_mean_scale(query_raw.reshape(tok_count, local_heads, HEAD_SIZE), query_gain),
            token_places,
        )
        * query_scale
    ).astype(jnp.bfloat16)
    projected_keys = apply_rotary(
        root_mean_scale(key_unnormed.reshape(tok_count, local_groups, HEAD_SIZE), key_norm_gain),
        token_places,
    ).astype(jnp.bfloat16)
    projected_values = value_unnormed.astype(jnp.bfloat16)
    key_value = jnp.stack(
        [projected_keys.reshape(tok_count, local_groups * HEAD_SIZE), projected_values]
    )
    pieces = [passed_along(key_value, "ctx", 1)]
    extended = jnp.concatenate(pieces + [key_value], axis=1)
    band_keys = extended[0].reshape(-1, local_groups, HEAD_SIZE)
    band_values = extended[1].reshape(-1, local_groups, HEAD_SIZE)
    block_rows = min(512, tok_count)
    grouped_queries = query_matrix.reshape(tok_count, local_groups, heads_per_group, HEAD_SIZE)
    outputs = []
    for block_index in range(tok_count // block_rows):
        first_row = block_index * block_rows
        query_block = grouped_queries[first_row : first_row + block_rows]
        key_block = band_keys[first_row : first_row + block_rows + WINDOW_SPAN]
        value_block = band_values[first_row : first_row + block_rows + WINDOW_SPAN]
        scores = jnp.einsum(
            "qjgd,kjd->jgqk", query_block, key_block, preferred_element_type=jnp.float32
        )
        query_spots = token_places[first_row : first_row + block_rows]
        key_spots = (
            ctx_index * tok_count
            - WINDOW_SPAN
            + first_row
            + jnp.arange(block_rows + WINDOW_SPAN, dtype=jnp.int32)
        )
        allowed = (
            (key_spots[None, :] <= query_spots[:, None])
            & (key_spots[None, :] > query_spots[:, None] - WINDOW_SPAN)
            & (key_spots[None, :] >= 0)
        )
        scores = jnp.where(allowed, scores, mask_value)
        row_max = jnp.max(scores, axis=-1, keepdims=True)
        weights = jnp.exp(scores - row_max)
        row_sum = jnp.sum(weights, axis=-1, keepdims=True)
        probabilities = (weights / row_sum).astype(jnp.bfloat16)
        mixed = jnp.einsum(
            "jgqk,kjd->qjgd", probabilities, value_block, preferred_element_type=jnp.float32
        )
        outputs.append(mixed.astype(jnp.bfloat16).reshape(block_rows, local_heads * HEAD_SIZE))
    attended = jnp.concatenate(outputs, axis=0)

    by_core = attended.reshape(chips, 2, rows, attended.shape[-1])
    attended_other = lax.dynamic_index_in_dim(by_core, 1 - core, 1, keepdims=False)
    attended_mine = lax.dynamic_index_in_dim(by_core, core, 1, keepdims=False)

    def out_project(part):
        part = part.reshape(chips * rows, part.shape[-1])
        return jnp.dot(part, out_weight, preferred_element_type=jnp.float32).astype(jnp.bfloat16)

    sent = rotated(out_project(attended_other), "core", 1)
    pair_sum = (
        out_project(attended_mine).astype(jnp.float32) + sent.astype(jnp.float32)
    ).astype(jnp.bfloat16)
    summed = lax.psum_scatter(
        pair_sum, "hc", scatter_dimension=0, tiled=True
    ).astype(jnp.float32)
    result = own_rows + root_mean_scale(summed, post_gain)
    return result.astype(jnp.bfloat16)


def solution(mesh):
    ctx_size, head_size = mesh.devices.shape
    view = Mesh(
        mesh.devices.reshape(ctx_size, head_size // 2, 2), ("ctx", "hc", "core")
    )
    rows_spec = P(("ctx", "hc", "core"), None)
    cols_spec = P("ctx", ("hc", "core"))
    return jax.shard_map(
        body,
        mesh=view,
        in_specs=(
            rows_spec,
            P(),
            cols_spec,
            cols_spec,
            cols_spec,
            P(),
            P(),
            P(("hc", "core", "ctx"), None),
            P(),
        ),
        out_specs=rows_spec,
        check_vma=False,
    )
```

```python
import jax
import jax.numpy as jnp
from jax import lax
from jax.sharding import Mesh, PartitionSpec as P

HEAD_SIZE = 128
WINDOW_SPAN = 1024


norm_eps = 1e-06
query_scale = 168.0 ** (-0.5)
rope_base = 10000.0
mask_value = -1e30
CTX = ("cx", "cy")
HEAD = ("hc", "core")


def passed_along(shard, axis, by):
    count = lax.axis_size(axis)
    pairs = [(i, i + by) for i in range(count) if 0 <= i + by < count]
    return lax.ppermute(shard, axis, pairs)


def rotated(shard, axis, by):
    count = lax.axis_size(axis)
    pairs = [(i, (i + by) % count) for i in range(count)]
    return lax.ppermute(shard, axis, pairs)


def placed(parts, me, count):
    stacked = jnp.zeros((count,) + parts[0].shape, parts[0].dtype)
    for i, part in enumerate(parts):
        stacked = lax.dynamic_update_index_in_dim(stacked, part, (me + i) % count, 0)
    return stacked


def gathered_over_ctx(piece):
    cy = lax.axis_index("cy")
    cx = lax.axis_index("cx")
    pair = placed([piece, rotated(piece, "cy", 1)], cy, 2)
    from_left = rotated(pair, "cx", 1)
    from_right = rotated(pair, "cx", -1)
    far = jnp.stack([rotated(from_left[0], "cx", 1), rotated(from_right[1], "cx", -1)])
    ring = placed([pair, from_right, far, from_left], cx, 4)
    return ring.reshape((8 * piece.shape[0],) + piece.shape[1:])


def root_mean_scale(values, scaling):
    mean_sq = jnp.mean(values * values, axis=-1, keepdims=True)
    return values * lax.rsqrt(mean_sq + norm_eps) * scaling


def apply_rotary(values, token_places):
    full_width = values.shape[-1]
    half_width = full_width // 2
    frequency = rope_base ** (-jnp.arange(half_width, dtype=jnp.float32) * 2.0 / full_width)
    angles = token_places.astype(jnp.float32)[:, None] * frequency[None, :]
    cosine = jnp.cos(angles)[:, None, :]
    sine_part = jnp.sin(angles)[:, None, :]
    lower_half = values[..., :half_width]
    upper_half = values[..., half_width:]
    return jnp.concatenate(
        [
            lower_half * cosine - upper_half * sine_part,
            upper_half * cosine + lower_half * sine_part,
        ],
        axis=-1,
    )


def body(
    hidden_in,
    pre_gain,
    w_query,
    w_key,
    value_weight,
    query_gain,
    key_norm_gain,
    w_output,
    post_gain,
):
    own_rows = hidden_in.astype(jnp.float32)
    q_cols = w_query.shape[1]
    k_cols = w_key.shape[1]
    w_in = gathered_over_ctx(jnp.concatenate([w_query, w_key, value_weight], axis=1))
    out_weight = gathered_over_ctx(w_output)

    raw_rows = lax.all_gather(hidden_in, HEAD, axis=0, tiled=True)
    normed = root_mean_scale(raw_rows.astype(jnp.float32), pre_gain).astype(jnp.bfloat16)
    tok_count = normed.shape[0]
    projected = jnp.dot(normed, w_in, preferred_element_type=jnp.float32)
    query_raw = projected[:, :q_cols]
    key_unnormed = projected[:, q_cols : q_cols + k_cols]
    value_unnormed = projected[:, q_cols + k_cols :]

    local_heads = q_cols // HEAD_SIZE
    local_groups = k_cols // HEAD_SIZE
    heads_per_group = local_heads // local_groups
    ctx_index = lax.axis_index(CTX)
    token_places = ctx_index * tok_count + jnp.arange(tok_count, dtype=jnp.int32)
    query_matrix = (
        apply_rotary(
            root_mean_scale(query_raw.reshape(tok_count, local_heads, HEAD_SIZE), query_gain),
            token_places,
        )
        * query_scale
    ).astype(jnp.bfloat16)
    projected_keys = apply_rotary(
        root_mean_scale(key_unnormed.reshape(tok_count, local_groups, HEAD_SIZE), key_norm_gain),
        token_places,
    ).astype(jnp.bfloat16)
    projected_values = value_unnormed.astype(jnp.bfloat16)
    key_value = jnp.stack(
        [projected_keys.reshape(tok_count, local_groups * HEAD_SIZE), projected_values]
    )
    pieces = [passed_along(key_value, CTX, 1)]
    extended = jnp.concatenate(pieces + [key_value], axis=1)
    band_keys = extended[0].reshape(-1, local_groups, HEAD_SIZE)
    band_values = extended[1].reshape(-1, local_groups, HEAD_SIZE)
    block_rows = min(512, tok_count)
    grouped_queries = query_matrix.reshape(tok_count, local_groups, heads_per_group, HEAD_SIZE)
    outputs = []
    for block_index in range(tok_count // block_rows):
        first_row = block_index * block_rows
        query_block = grouped_queries[first_row : first_row + block_rows]
        key_block = band_keys[first_row : first_row + block_rows + WINDOW_SPAN]
        value_block = band_values[first_row : first_row + block_rows + WINDOW_SPAN]
        scores = jnp.einsum(
            "qjgd,kjd->jgqk", query_block, key_block, preferred_element_type=jnp.float32
        )
        query_spots = token_places[first_row : first_row + block_rows]
        key_spots = (
            ctx_index * tok_count
            - WINDOW_SPAN
            + first_row
            + jnp.arange(block_rows + WINDOW_SPAN, dtype=jnp.int32)
        )
        allowed = (
            (key_spots[None, :] <= query_spots[:, None])
            & (key_spots[None, :] > query_spots[:, None] - WINDOW_SPAN)
            & (key_spots[None, :] >= 0)
        )
        scores = jnp.where(allowed, scores, mask_value)
        row_max = jnp.max(scores, axis=-1, keepdims=True)
        weights = jnp.exp(scores - row_max)
        row_sum = jnp.sum(weights, axis=-1, keepdims=True)
        probabilities = (weights / row_sum).astype(jnp.bfloat16)
        mixed = jnp.einsum(
            "jgqk,kjd->qjgd", probabilities, value_block, preferred_element_type=jnp.float32
        )
        outputs.append(mixed.astype(jnp.bfloat16).reshape(block_rows, local_heads * HEAD_SIZE))
    attended = jnp.concatenate(outputs, axis=0)

    partial_value = jnp.dot(attended, out_weight, preferred_element_type=jnp.float32).astype(
        jnp.bfloat16
    )
    summed = lax.psum_scatter(
        partial_value, HEAD, scatter_dimension=0, tiled=True
    ).astype(jnp.float32)
    result = own_rows + root_mean_scale(summed, post_gain)
    return result.astype(jnp.bfloat16)


def solution(mesh):
    ctx_size, head_size = mesh.devices.shape
    view = Mesh(
        mesh.devices.reshape(ctx_size // 2, 2, head_size // 2, 2), CTX + HEAD
    )
    rows_spec = P(CTX + HEAD, None)
    cols_spec = P(CTX, HEAD)
    return jax.shard_map(
        body,
        mesh=view,
        in_specs=(
            rows_spec,
            P(),
            cols_spec,
            cols_spec,
            cols_spec,
            P(),
            P(),
            P(HEAD + CTX, None),
            P(),
        ),
        out_specs=rows_spec,
        check_vma=False,
    )
```

```python
import jax
import jax.numpy as jnp
from jax import lax
from jax.sharding import Mesh, PartitionSpec as P

HEAD_SIZE = 128
WINDOW_SPAN = 1024


norm_eps = 1e-06
query_scale = 168.0 ** (-0.5)
rope_base = 10000.0
mask_value = -1e30
CTX = ("cx", "cy")
HEAD = ("hc", "core")


def passed_along(shard, axis, by):
    count = lax.axis_size(axis)
    pairs = [(i, i + by) for i in range(count) if 0 <= i + by < count]
    return lax.ppermute(shard, axis, pairs)


def rotated(shard, axis, by):
    count = lax.axis_size(axis)
    pairs = [(i, (i + by) % count) for i in range(count)]
    return lax.ppermute(shard, axis, pairs)


def placed(parts, me, count):
    stacked = jnp.zeros((count,) + parts[0].shape, parts[0].dtype)
    for i, part in enumerate(parts):
        stacked = lax.dynamic_update_index_in_dim(stacked, part, (me + i) % count, 0)
    return stacked


def ring_over_cx(piece):
    half = piece.shape[0] // 2
    from_left = rotated(piece, "cx", 1)
    from_right = rotated(piece, "cx", -1)
    far = jnp.concatenate(
        [rotated(from_left[:half], "cx", 1), rotated(from_right[half:], "cx", -1)]
    )
    return [piece, from_right, far, from_left]


def gathered_over_ctx(piece):
    cy = lax.axis_index("cy")
    cx = lax.axis_index("cx")
    own = ring_over_cx(piece)
    partner = ring_over_cx(rotated(piece, "cy", 1))
    pairs = [placed([a, b], cy, 2) for a, b in zip(own, partner)]
    ring = placed(pairs, cx, 4)
    return ring.reshape((8 * piece.shape[0],) + piece.shape[1:])


def root_mean_scale(values, scaling):
    mean_sq = jnp.mean(values * values, axis=-1, keepdims=True)
    return values * lax.rsqrt(mean_sq + norm_eps) * scaling


def apply_rotary(values, token_places):
    full_width = values.shape[-1]
    half_width = full_width // 2
    frequency = rope_base ** (-jnp.arange(half_width, dtype=jnp.float32) * 2.0 / full_width)
    angles = token_places.astype(jnp.float32)[:, None] * frequency[None, :]
    cosine = jnp.cos(angles)[:, None, :]
    sine_part = jnp.sin(angles)[:, None, :]
    lower_half = values[..., :half_width]
    upper_half = values[..., half_width:]
    return jnp.concatenate(
        [
            lower_half * cosine - upper_half * sine_part,
            upper_half * cosine + lower_half * sine_part,
        ],
        axis=-1,
    )


def body(
    hidden_in,
    pre_gain,
    w_query,
    w_key,
    value_weight,
    query_gain,
    key_norm_gain,
    w_output,
    post_gain,
):
    own_rows = hidden_in.astype(jnp.float32)
    q_cols = w_query.shape[1]
    k_cols = w_key.shape[1]
    w_in = gathered_over_ctx(jnp.concatenate([w_query, w_key, value_weight], axis=1))

    raw_rows = lax.all_gather(hidden_in, HEAD, axis=0, tiled=True)
    normed = root_mean_scale(raw_rows.astype(jnp.float32), pre_gain).astype(jnp.bfloat16)
    tok_count = normed.shape[0]
    projected = jnp.dot(normed, w_in, preferred_element_type=jnp.float32)
    projected, w_output = lax.optimization_barrier((projected, w_output))
    out_weight = gathered_over_ctx(w_output)
    query_raw = projected[:, :q_cols]
    key_unnormed = projected[:, q_cols : q_cols + k_cols]
    value_unnormed = projected[:, q_cols + k_cols :]

    local_heads = q_cols // HEAD_SIZE
    local_groups = k_cols // HEAD_SIZE
    heads_per_group = local_heads // local_groups
    ctx_index = lax.axis_index(CTX)
    token_places = ctx_index * tok_count + jnp.arange(tok_count, dtype=jnp.int32)
    query_matrix = (
        apply_rotary(
            root_mean_scale(query_raw.reshape(tok_count, local_heads, HEAD_SIZE), query_gain),
            token_places,
        )
        * query_scale
    ).astype(jnp.bfloat16)
    projected_keys = apply_rotary(
        root_mean_scale(key_unnormed.reshape(tok_count, local_groups, HEAD_SIZE), key_norm_gain),
        token_places,
    ).astype(jnp.bfloat16)
    projected_values = value_unnormed.astype(jnp.bfloat16)
    key_value = jnp.stack(
        [projected_keys.reshape(tok_count, local_groups * HEAD_SIZE), projected_values]
    )
    pieces = [passed_along(key_value, CTX, 1)]
    extended = jnp.concatenate(pieces + [key_value], axis=1)
    band_keys = extended[0].reshape(-1, local_groups, HEAD_SIZE)
    band_values = extended[1].reshape(-1, local_groups, HEAD_SIZE)
    block_rows = min(512, tok_count)
    grouped_queries = query_matrix.reshape(tok_count, local_groups, heads_per_group, HEAD_SIZE)
    outputs = []
    for block_index in range(tok_count // block_rows):
        first_row = block_index * block_rows
        query_block = grouped_queries[first_row : first_row + block_rows]
        key_block = band_keys[first_row : first_row + block_rows + WINDOW_SPAN]
        value_block = band_values[first_row : first_row + block_rows + WINDOW_SPAN]
        scores = jnp.einsum(
            "qjgd,kjd->jgqk", query_block, key_block, preferred_element_type=jnp.float32
        )
        query_spots = token_places[first_row : first_row + block_rows]
        key_spots = (
            ctx_index * tok_count
            - WINDOW_SPAN
            + first_row
            + jnp.arange(block_rows + WINDOW_SPAN, dtype=jnp.int32)
        )
        allowed = (
            (key_spots[None, :] <= query_spots[:, None])
            & (key_spots[None, :] > query_spots[:, None] - WINDOW_SPAN)
            & (key_spots[None, :] >= 0)
        )
        scores = jnp.where(allowed, scores, mask_value)
        row_max = jnp.max(scores, axis=-1, keepdims=True)
        weights = jnp.exp(scores - row_max)
        row_sum = jnp.sum(weights, axis=-1, keepdims=True)
        probabilities = (weights / row_sum).astype(jnp.bfloat16)
        mixed = jnp.einsum(
            "jgqk,kjd->qjgd", probabilities, value_block, preferred_element_type=jnp.float32
        )
        outputs.append(mixed.astype(jnp.bfloat16).reshape(block_rows, local_heads * HEAD_SIZE))
    attended = jnp.concatenate(outputs, axis=0)

    partial_value = jnp.dot(attended, out_weight, preferred_element_type=jnp.float32).astype(
        jnp.bfloat16
    )
    summed = lax.psum_scatter(
        partial_value, HEAD, scatter_dimension=0, tiled=True
    ).astype(jnp.float32)
    result = own_rows + root_mean_scale(summed, post_gain)
    return result.astype(jnp.bfloat16)


def solution(mesh):
    ctx_size, head_size = mesh.devices.shape
    view = Mesh(
        mesh.devices.reshape(ctx_size // 2, 2, head_size // 2, 2), CTX + HEAD
    )
    rows_spec = P(CTX + HEAD, None)
    cols_spec = P(CTX, HEAD)
    return jax.shard_map(
        body,
        mesh=view,
        in_specs=(
            rows_spec,
            P(),
            cols_spec,
            cols_spec,
            cols_spec,
            P(),
            P(),
            P(HEAD + CTX, None),
            P(),
        ),
        out_specs=rows_spec,
        check_vma=False,
    )
```

```python
import jax
import jax.numpy as jnp
from jax import lax
from jax.sharding import Mesh, PartitionSpec as P

HEAD_SIZE = 128
WINDOW_SPAN = 1024


norm_eps = 1e-06
query_scale = 168.0 ** (-0.5)
rope_base = 10000.0
mask_value = -1e30
CTX = ("cx", "cy")
HEAD = ("ylo", "z", "core")


def passed_along(shard, axis, by):
    count = lax.axis_size(axis)
    pairs = [(i, i + by) for i in range(count) if 0 <= i + by < count]
    return lax.ppermute(shard, axis, pairs)


def rotated(shard, axis, by):
    count = lax.axis_size(axis)
    pairs = [(i, (i + by) % count) for i in range(count)]
    return lax.ppermute(shard, axis, pairs)


def placed(parts, me, count):
    stacked = jnp.zeros((count,) + parts[0].shape, parts[0].dtype)
    for i, part in enumerate(parts):
        stacked = lax.dynamic_update_index_in_dim(stacked, part, (me + i) % count, 0)
    return stacked


def ring_over_cx(piece):
    half = piece.shape[0] // 2
    from_left = rotated(piece, "cx", 1)
    from_right = rotated(piece, "cx", -1)
    far = jnp.concatenate(
        [rotated(from_left[:half], "cx", 1), rotated(from_right[half:], "cx", -1)]
    )
    return [piece, from_right, far, from_left]


def gathered_over_ctx(piece):
    cy = lax.axis_index("cy")
    cx = lax.axis_index("cx")
    own = ring_over_cx(piece)
    partner = ring_over_cx(rotated(piece, "cy", 1))
    pairs = [placed([a, b], cy, 2) for a, b in zip(own, partner)]
    ring = placed(pairs, cx, 4)
    return ring.reshape((8 * piece.shape[0],) + piece.shape[1:])


def reduced_over_head(partial, core_axis_len=2, z_len=4):
    core = lax.axis_index("core")
    width = partial.shape[-1]
    rows = partial.shape[0] // (2 * z_len * core_axis_len)
    blocks = partial.reshape(2, z_len, core_axis_len, rows, width)
    give = lax.dynamic_index_in_dim(blocks, 1 - core, 2, keepdims=False)
    keep = lax.dynamic_index_in_dim(blocks, core, 2, keepdims=False)
    pair = keep.astype(jnp.float32) + rotated(give, "core", 1).astype(jnp.float32)
    pair = pair.astype(jnp.bfloat16)
    z = lax.axis_index("z")
    half = width // 2
    sums = []
    for direction, cols in ((1, slice(0, half)), (-1, slice(half, width))):
        part = pair[:, :, :, cols]
        acc = None
        for step in range(z_len - 1):
            chunk = (z - direction * (step + 1)) % z_len
            mine = lax.dynamic_index_in_dim(part, chunk, 1, keepdims=False).astype(jnp.float32)
            if acc is not None:
                mine = mine + acc
            acc = rotated(mine.astype(jnp.bfloat16), "z", direction).astype(jnp.float32)
        sums.append(lax.dynamic_index_in_dim(part, z, 1, keepdims=False).astype(jnp.float32) + acc)
    by_plane = jnp.concatenate(sums, axis=-1)
    y = lax.axis_index("ylo")
    give = lax.dynamic_index_in_dim(by_plane, 1 - y, 0, keepdims=False)
    keep = lax.dynamic_index_in_dim(by_plane, y, 0, keepdims=False)
    return keep + rotated(give.astype(jnp.bfloat16), "ylo", 1).astype(jnp.float32)


def root_mean_scale(values, scaling):
    mean_sq = jnp.mean(values * values, axis=-1, keepdims=True)
    return values * lax.rsqrt(mean_sq + norm_eps) * scaling


def apply_rotary(values, token_places):
    full_width = values.shape[-1]
    half_width = full_width // 2
    frequency = rope_base ** (-jnp.arange(half_width, dtype=jnp.float32) * 2.0 / full_width)
    angles = token_places.astype(jnp.float32)[:, None] * frequency[None, :]
    cosine = jnp.cos(angles)[:, None, :]
    sine_part = jnp.sin(angles)[:, None, :]
    lower_half = values[..., :half_width]
    upper_half = values[..., half_width:]
    return jnp.concatenate(
        [
            lower_half * cosine - upper_half * sine_part,
            upper_half * cosine + lower_half * sine_part,
        ],
        axis=-1,
    )


def body(
    hidden_in,
    pre_gain,
    w_query,
    w_key,
    value_weight,
    query_gain,
    key_norm_gain,
    w_output,
    post_gain,
):
    own_rows = hidden_in.astype(jnp.float32)
    q_cols = w_query.shape[1]
    k_cols = w_key.shape[1]
    w_in = gathered_over_ctx(jnp.concatenate([w_query, w_key, value_weight], axis=1))

    raw_rows = lax.all_gather(hidden_in, HEAD, axis=0, tiled=True)
    normed = root_mean_scale(raw_rows.astype(jnp.float32), pre_gain).astype(jnp.bfloat16)
    tok_count = normed.shape[0]
    projected = jnp.dot(normed, w_in, preferred_element_type=jnp.float32)
    projected, w_output = lax.optimization_barrier((projected, w_output))
    out_weight = gathered_over_ctx(w_output)
    query_raw = projected[:, :q_cols]
    key_unnormed = projected[:, q_cols : q_cols + k_cols]
    value_unnormed = projected[:, q_cols + k_cols :]

    local_heads = q_cols // HEAD_SIZE
    local_groups = k_cols // HEAD_SIZE
    heads_per_group = local_heads // local_groups
    ctx_index = lax.axis_index(CTX)
    token_places = ctx_index * tok_count + jnp.arange(tok_count, dtype=jnp.int32)
    query_matrix = (
        apply_rotary(
            root_mean_scale(query_raw.reshape(tok_count, local_heads, HEAD_SIZE), query_gain),
            token_places,
        )
        * query_scale
    ).astype(jnp.bfloat16)
    projected_keys = apply_rotary(
        root_mean_scale(key_unnormed.reshape(tok_count, local_groups, HEAD_SIZE), key_norm_gain),
        token_places,
    ).astype(jnp.bfloat16)
    projected_values = value_unnormed.astype(jnp.bfloat16)
    key_value = jnp.stack(
        [projected_keys.reshape(tok_count, local_groups * HEAD_SIZE), projected_values]
    )
    pieces = [passed_along(key_value, CTX, 1)]
    extended = jnp.concatenate(pieces + [key_value], axis=1)
    band_keys = extended[0].reshape(-1, local_groups, HEAD_SIZE)
    band_values = extended[1].reshape(-1, local_groups, HEAD_SIZE)
    block_rows = min(512, tok_count)
    grouped_queries = query_matrix.reshape(tok_count, local_groups, heads_per_group, HEAD_SIZE)
    outputs = []
    for block_index in range(tok_count // block_rows):
        first_row = block_index * block_rows
        query_block = grouped_queries[first_row : first_row + block_rows]
        key_block = band_keys[first_row : first_row + block_rows + WINDOW_SPAN]
        value_block = band_values[first_row : first_row + block_rows + WINDOW_SPAN]
        scores = jnp.einsum(
            "qjgd,kjd->jgqk", query_block, key_block, preferred_element_type=jnp.float32
        )
        query_spots = token_places[first_row : first_row + block_rows]
        key_spots = (
            ctx_index * tok_count
            - WINDOW_SPAN
            + first_row
            + jnp.arange(block_rows + WINDOW_SPAN, dtype=jnp.int32)
        )
        allowed = (
            (key_spots[None, :] <= query_spots[:, None])
            & (key_spots[None, :] > query_spots[:, None] - WINDOW_SPAN)
            & (key_spots[None, :] >= 0)
        )
        scores = jnp.where(allowed, scores, mask_value)
        row_max = jnp.max(scores, axis=-1, keepdims=True)
        weights = jnp.exp(scores - row_max)
        row_sum = jnp.sum(weights, axis=-1, keepdims=True)
        probabilities = (weights / row_sum).astype(jnp.bfloat16)
        mixed = jnp.einsum(
            "jgqk,kjd->qjgd", probabilities, value_block, preferred_element_type=jnp.float32
        )
        outputs.append(mixed.astype(jnp.bfloat16).reshape(block_rows, local_heads * HEAD_SIZE))
    attended = jnp.concatenate(outputs, axis=0)

    partial_value = jnp.dot(attended, out_weight, preferred_element_type=jnp.float32).astype(
        jnp.bfloat16
    )
    summed = reduced_over_head(partial_value)
    result = own_rows + root_mean_scale(summed, post_gain)
    return result.astype(jnp.bfloat16)


def solution(mesh):
    ctx_size, head_size = mesh.devices.shape
    view = Mesh(
        mesh.devices.reshape(ctx_size // 2, 2, 2, head_size // 4, 2), CTX + HEAD
    )
    rows_spec = P(CTX + HEAD, None)
    cols_spec = P(CTX, HEAD)
    return jax.shard_map(
        body,
        mesh=view,
        in_specs=(
            rows_spec,
            P(),
            cols_spec,
            cols_spec,
            cols_spec,
            P(),
            P(),
            P(HEAD + CTX, None),
            P(),
        ),
        out_specs=rows_spec,
        check_vma=False,
    )
```

```python
import jax
import jax.numpy as jnp
from jax import lax
from jax.sharding import Mesh, PartitionSpec as P

HEAD_SIZE = 128
WINDOW_SPAN = 1024


norm_eps = 1e-06
query_scale = 168.0 ** (-0.5)
rope_base = 10000.0
mask_value = -1e30
CTX = ("cx", "cy")
HEAD = ("hc", "core")


def passed_along(shard, axis, by):
    count = lax.axis_size(axis)
    pairs = [(i, i + by) for i in range(count) if 0 <= i + by < count]
    return lax.ppermute(shard, axis, pairs)


def rotated(shard, axis, by):
    count = lax.axis_size(axis)
    pairs = [(i, (i + by) % count) for i in range(count)]
    return lax.ppermute(shard, axis, pairs)


def placed(parts, me, count):
    stacked = jnp.zeros((count,) + parts[0].shape, parts[0].dtype)
    for i, part in enumerate(parts):
        stacked = lax.dynamic_update_index_in_dim(stacked, part, (me + i) % count, 0)
    return stacked


def ring_over_cx(piece):
    half = piece.shape[0] // 2
    from_left = rotated(piece, "cx", 1)
    from_right = rotated(piece, "cx", -1)
    far = jnp.concatenate(
        [rotated(from_left[:half], "cx", 1), rotated(from_right[half:], "cx", -1)]
    )
    return [piece, from_right, far, from_left]


def gathered_over_ctx(piece):
    cy = lax.axis_index("cy")
    cx = lax.axis_index("cx")
    own = ring_over_cx(piece)
    partner = ring_over_cx(rotated(piece, "cy", 1))
    pairs = [placed([a, b], cy, 2) for a, b in zip(own, partner)]
    ring = placed(pairs, cx, 4)
    return ring.reshape((8 * piece.shape[0],) + piece.shape[1:])


def root_mean_scale(values, scaling):
    mean_sq = jnp.mean(values * values, axis=-1, keepdims=True)
    return values * lax.rsqrt(mean_sq + norm_eps) * scaling


def apply_rotary(values, token_places):
    full_width = values.shape[-1]
    half_width = full_width // 2
    frequency = rope_base ** (-jnp.arange(half_width, dtype=jnp.float32) * 2.0 / full_width)
    angles = token_places.astype(jnp.float32)[:, None] * frequency[None, :]
    cosine = jnp.cos(angles)[:, None, :]
    sine_part = jnp.sin(angles)[:, None, :]
    lower_half = values[..., :half_width]
    upper_half = values[..., half_width:]
    return jnp.concatenate(
        [
            lower_half * cosine - upper_half * sine_part,
            upper_half * cosine + lower_half * sine_part,
        ],
        axis=-1,
    )


def body(
    hidden_in,
    pre_gain,
    w_query,
    w_key,
    value_weight,
    query_gain,
    key_norm_gain,
    w_output,
    post_gain,
):
    own_rows = hidden_in.astype(jnp.float32)
    q_cols = w_query.shape[1]
    k_cols = w_key.shape[1]
    w_in = gathered_over_ctx(jnp.concatenate([w_query, w_key, value_weight], axis=1))

    raw_rows = lax.all_gather(hidden_in, HEAD, axis=0, tiled=True)
    raw_rows, w_output = lax.optimization_barrier((raw_rows, w_output))
    out_weight = lax.all_gather(w_output, CTX, axis=0, tiled=True)
    normed = root_mean_scale(raw_rows.astype(jnp.float32), pre_gain).astype(jnp.bfloat16)
    tok_count = normed.shape[0]
    projected = jnp.dot(normed, w_in, preferred_element_type=jnp.float32)
    query_raw = projected[:, :q_cols]
    key_unnormed = projected[:, q_cols : q_cols + k_cols]
    value_unnormed = projected[:, q_cols + k_cols :]

    local_heads = q_cols // HEAD_SIZE
    local_groups = k_cols // HEAD_SIZE
    heads_per_group = local_heads // local_groups
    ctx_index = lax.axis_index(CTX)
    token_places = ctx_index * tok_count + jnp.arange(tok_count, dtype=jnp.int32)
    query_matrix = (
        apply_rotary(
            root_mean_scale(query_raw.reshape(tok_count, local_heads, HEAD_SIZE), query_gain),
            token_places,
        )
        * query_scale
    ).astype(jnp.bfloat16)
    projected_keys = apply_rotary(
        root_mean_scale(key_unnormed.reshape(tok_count, local_groups, HEAD_SIZE), key_norm_gain),
        token_places,
    ).astype(jnp.bfloat16)
    projected_values = value_unnormed.astype(jnp.bfloat16)
    key_value = jnp.stack(
        [projected_keys.reshape(tok_count, local_groups * HEAD_SIZE), projected_values]
    )
    pieces = [passed_along(key_value, CTX, 1)]
    extended = jnp.concatenate(pieces + [key_value], axis=1)
    band_keys = extended[0].reshape(-1, local_groups, HEAD_SIZE)
    band_values = extended[1].reshape(-1, local_groups, HEAD_SIZE)
    block_rows = min(512, tok_count)
    grouped_queries = query_matrix.reshape(tok_count, local_groups, heads_per_group, HEAD_SIZE)
    outputs = []
    for block_index in range(tok_count // block_rows):
        first_row = block_index * block_rows
        query_block = grouped_queries[first_row : first_row + block_rows]
        key_block = band_keys[first_row : first_row + block_rows + WINDOW_SPAN]
        value_block = band_values[first_row : first_row + block_rows + WINDOW_SPAN]
        scores = jnp.einsum(
            "qjgd,kjd->jgqk", query_block, key_block, preferred_element_type=jnp.float32
        )
        query_spots = token_places[first_row : first_row + block_rows]
        key_spots = (
            ctx_index * tok_count
            - WINDOW_SPAN
            + first_row
            + jnp.arange(block_rows + WINDOW_SPAN, dtype=jnp.int32)
        )
        allowed = (
            (key_spots[None, :] <= query_spots[:, None])
            & (key_spots[None, :] > query_spots[:, None] - WINDOW_SPAN)
            & (key_spots[None, :] >= 0)
        )
        scores = jnp.where(allowed, scores, mask_value)
        row_max = jnp.max(scores, axis=-1, keepdims=True)
        weights = jnp.exp(scores - row_max)
        row_sum = jnp.sum(weights, axis=-1, keepdims=True)
        probabilities = (weights / row_sum).astype(jnp.bfloat16)
        mixed = jnp.einsum(
            "jgqk,kjd->qjgd", probabilities, value_block, preferred_element_type=jnp.float32
        )
        outputs.append(mixed.astype(jnp.bfloat16).reshape(block_rows, local_heads * HEAD_SIZE))
    attended = jnp.concatenate(outputs, axis=0)

    partial_value = jnp.dot(attended, out_weight, preferred_element_type=jnp.float32).astype(
        jnp.bfloat16
    )
    summed = lax.psum_scatter(
        partial_value, HEAD, scatter_dimension=0, tiled=True
    ).astype(jnp.float32)
    result = own_rows + root_mean_scale(summed, post_gain)
    return result.astype(jnp.bfloat16)


def solution(mesh):
    ctx_size, head_size = mesh.devices.shape
    view = Mesh(
        mesh.devices.reshape(ctx_size // 2, 2, head_size // 2, 2), CTX + HEAD
    )
    rows_spec = P(CTX + HEAD, None)
    cols_spec = P(CTX, HEAD)
    return jax.shard_map(
        body,
        mesh=view,
        in_specs=(
            rows_spec,
            P(),
            cols_spec,
            cols_spec,
            cols_spec,
            P(),
            P(),
            P(HEAD + CTX, None),
            P(),
        ),
        out_specs=rows_spec,
        check_vma=False,
    )
```

```python
import jax
import jax.numpy as jnp
from jax import lax
from jax.sharding import Mesh, PartitionSpec as P


HEAD_SIZE = 128
WINDOW_SPAN = 1024


norm_eps = 1e-06
query_scale = 168.0 ** (-0.5)
rope_base = 10000.0
mask_value = -1e30
CTX = ("cx", "cy")
HEAD = ("hc", "core")


def passed_along(shard, axis, by):
    count = lax.axis_size(axis)
    pairs = [(i, i + by) for i in range(count) if 0 <= i + by < count]
    return lax.ppermute(shard, axis, pairs)


def rotated(shard, axis, by):
    count = lax.axis_size(axis)
    pairs = [(i, (i + by) % count) for i in range(count)]
    return lax.ppermute(shard, axis, pairs)


def placed(parts, me, count):
    stacked = jnp.zeros((count,) + parts[0].shape, parts[0].dtype)
    for i, part in enumerate(parts):
        stacked = lax.dynamic_update_index_in_dim(stacked, part, (me + i) % count, 0)
    return stacked


def ring_over_cx(piece):
    half = piece.shape[0] // 2
    from_left = rotated(piece, "cx", 1)
    from_right = rotated(piece, "cx", -1)
    far = jnp.concatenate(
        [rotated(from_left[:half], "cx", 1), rotated(from_right[half:], "cx", -1)]
    )
    return [piece, from_right, far, from_left]


def gathered_over_ctx(piece):
    cy = lax.axis_index("cy")
    cx = lax.axis_index("cx")
    own = ring_over_cx(piece)
    partner = ring_over_cx(rotated(piece, "cy", 1))
    pairs = [placed([a, b], cy, 2) for a, b in zip(own, partner)]
    ring = placed(pairs, cx, 4)
    return ring.reshape((8 * piece.shape[0],) + piece.shape[1:])


def gathered_directly(piece, axis):
    count = lax.axis_size(axis)
    me = lax.axis_index(axis)
    parts = [piece] + [rotated(piece, axis, by) for by in range(count - 1, 0, -1)]
    stacked = placed(parts, me, count)
    return stacked.reshape((count * piece.shape[0],) + piece.shape[1:])


def root_mean_scale(values, scaling):
    mean_sq = jnp.mean(values * values, axis=-1, keepdims=True)
    return values * lax.rsqrt(mean_sq + norm_eps) * scaling


def apply_rotary(values, token_places):
    full_width = values.shape[-1]
    half_width = full_width // 2
    frequency = rope_base ** (-jnp.arange(half_width, dtype=jnp.float32) * 2.0 / full_width)
    angles = token_places.astype(jnp.float32)[:, None] * frequency[None, :]
    cosine = jnp.cos(angles)[:, None, :]
    sine_part = jnp.sin(angles)[:, None, :]
    lower_half = values[..., :half_width]
    upper_half = values[..., half_width:]
    return jnp.concatenate(
        [
            lower_half * cosine - upper_half * sine_part,
            upper_half * cosine + lower_half * sine_part,
        ],
        axis=-1,
    )


def layer(
    hidden_in,
    pre_gain,
    w_query,
    w_key,
    value_weight,
    query_gain,
    key_norm_gain,
    w_output,
    post_gain,
):
    own_rows = hidden_in.astype(jnp.float32)
    q_cols = w_query.shape[1]
    k_cols = w_key.shape[1]
    w_in = gathered_over_ctx(jnp.concatenate([w_query, w_key, value_weight], axis=1))

    w_in, w_output = lax.optimization_barrier((w_in, w_output))
    out_weight = gathered_directly(w_output, CTX)
    raw_rows = lax.all_gather(hidden_in, HEAD, axis=0, tiled=True)
    tok_count = raw_rows.shape[0]
    normed = root_mean_scale(raw_rows.astype(jnp.float32), pre_gain).astype(jnp.bfloat16)
    projected = jnp.dot(normed, w_in, preferred_element_type=jnp.float32)
    query_raw = projected[:, :q_cols]
    key_unnormed = projected[:, q_cols : q_cols + k_cols]
    value_unnormed = projected[:, q_cols + k_cols :]

    local_heads = q_cols // HEAD_SIZE
    local_groups = k_cols // HEAD_SIZE
    heads_per_group = local_heads // local_groups
    ctx_index = lax.axis_index(CTX)
    token_places = ctx_index * tok_count + jnp.arange(tok_count, dtype=jnp.int32)
    query_matrix = (
        apply_rotary(
            root_mean_scale(query_raw.reshape(tok_count, local_heads, HEAD_SIZE), query_gain),
            token_places,
        )
        * query_scale
    ).astype(jnp.bfloat16)
    projected_keys = apply_rotary(
        root_mean_scale(key_unnormed.reshape(tok_count, local_groups, HEAD_SIZE), key_norm_gain),
        token_places,
    ).astype(jnp.bfloat16)
    projected_values = value_unnormed.astype(jnp.bfloat16)
    key_value = jnp.stack(
        [projected_keys.reshape(tok_count, local_groups * HEAD_SIZE), projected_values]
    )
    pieces = [passed_along(key_value, CTX, 1)]
    extended = jnp.concatenate(pieces + [key_value], axis=1)
    band_keys = extended[0].reshape(-1, local_groups, HEAD_SIZE)
    band_values = extended[1].reshape(-1, local_groups, HEAD_SIZE)
    block_rows = min(512, tok_count)
    grouped_queries = query_matrix.reshape(tok_count, local_groups, heads_per_group, HEAD_SIZE)
    outputs = []
    for block_index in range(tok_count // block_rows):
        first_row = block_index * block_rows
        query_block = grouped_queries[first_row : first_row + block_rows]
        key_block = band_keys[first_row : first_row + block_rows + WINDOW_SPAN]
        value_block = band_values[first_row : first_row + block_rows + WINDOW_SPAN]
        scores = jnp.einsum(
            "qjgd,kjd->jgqk", query_block, key_block, preferred_element_type=jnp.float32
        )
        query_spots = token_places[first_row : first_row + block_rows]
        key_spots = (
            ctx_index * tok_count
            - WINDOW_SPAN
            + first_row
            + jnp.arange(block_rows + WINDOW_SPAN, dtype=jnp.int32)
        )
        allowed = (
            (key_spots[None, :] <= query_spots[:, None])
            & (key_spots[None, :] > query_spots[:, None] - WINDOW_SPAN)
            & (key_spots[None, :] >= 0)
        )
        scores = jnp.where(allowed, scores, mask_value)
        row_max = jnp.max(scores, axis=-1, keepdims=True)
        weights = jnp.exp(scores - row_max)
        row_sum = jnp.sum(weights, axis=-1, keepdims=True)
        probabilities = (weights / row_sum).astype(jnp.bfloat16)
        mixed = jnp.einsum(
            "jgqk,kjd->qjgd", probabilities, value_block, preferred_element_type=jnp.float32
        )
        outputs.append(mixed.astype(jnp.bfloat16).reshape(block_rows, local_heads * HEAD_SIZE))
    attended = jnp.concatenate(outputs, axis=0)

    partial_value = jnp.dot(attended, out_weight, preferred_element_type=jnp.float32).astype(
        jnp.bfloat16
    )
    summed = lax.psum_scatter(
        partial_value, HEAD, scatter_dimension=0, tiled=True
    ).astype(jnp.float32)
    result = own_rows + root_mean_scale(summed, post_gain)
    return result.astype(jnp.bfloat16)


def solution(mesh):
    ctx_size, head_size = mesh.devices.shape
    view = Mesh(
        mesh.devices.reshape(ctx_size // 2, 2, head_size // 2, 2), CTX + HEAD
    )
    rows_spec = P(CTX + HEAD, None)
    cols_spec = P(CTX, HEAD)
    return jax.shard_map(
        layer,
        mesh=view,
        in_specs=(
            rows_spec,
            P(),
            cols_spec,
            cols_spec,
            cols_spec,
            P(),
            P(),
            P(HEAD + CTX, None),
            P(),
        ),
        out_specs=rows_spec,
        check_vma=False,
    )
```

```python
import jax
import jax.numpy as jnp
from jax import lax
from jax.sharding import Mesh, PartitionSpec as P

HEAD_SIZE = 128
WINDOW_SPAN = 1024


norm_eps = 1e-06
query_scale = 168.0 ** (-0.5)
rope_base = 10000.0
mask_value = -1e30
CTX = ("cx", "cy")
HEAD = ("hc", "core")


def passed_along(shard, axis, by):
    count = lax.axis_size(axis)
    pairs = [(i, i + by) for i in range(count) if 0 <= i + by < count]
    return lax.ppermute(shard, axis, pairs)


def rotated(shard, axis, by):
    count = lax.axis_size(axis)
    pairs = [(i, (i + by) % count) for i in range(count)]
    return lax.ppermute(shard, axis, pairs)


def placed(parts, me, count):
    stacked = jnp.zeros((count,) + parts[0].shape, parts[0].dtype)
    for i, part in enumerate(parts):
        stacked = lax.dynamic_update_index_in_dim(stacked, part, (me + i) % count, 0)
    return stacked


def ring_over_cx(piece):
    half = piece.shape[0] // 2
    from_left = rotated(piece, "cx", 1)
    from_right = rotated(piece, "cx", -1)
    far = jnp.concatenate(
        [rotated(from_left[:half], "cx", 1), rotated(from_right[half:], "cx", -1)]
    )
    return [piece, from_right, far, from_left]


def gathered_over_ctx(piece):
    cy = lax.axis_index("cy")
    cx = lax.axis_index("cx")
    own = ring_over_cx(piece)
    partner = ring_over_cx(rotated(piece, "cy", 1))
    pairs = [placed([a, b], cy, 2) for a, b in zip(own, partner)]
    ring = placed(pairs, cx, 4)
    return ring.reshape((8 * piece.shape[0],) + piece.shape[1:])


def root_mean_scale(values, scaling):
    mean_sq = jnp.mean(values * values, axis=-1, keepdims=True)
    return values * lax.rsqrt(mean_sq + norm_eps) * scaling


def apply_rotary(values, token_places):
    full_width = values.shape[-1]
    half_width = full_width // 2
    frequency = rope_base ** (-jnp.arange(half_width, dtype=jnp.float32) * 2.0 / full_width)
    angles = token_places.astype(jnp.float32)[:, None] * frequency[None, :]
    cosine = jnp.cos(angles)[:, None, :]
    sine_part = jnp.sin(angles)[:, None, :]
    lower_half = values[..., :half_width]
    upper_half = values[..., half_width:]
    return jnp.concatenate(
        [
            lower_half * cosine - upper_half * sine_part,
            upper_half * cosine + lower_half * sine_part,
        ],
        axis=-1,
    )


def body(
    hidden_in,
    pre_gain,
    w_query,
    w_key,
    value_weight,
    query_gain,
    key_norm_gain,
    w_output,
    post_gain,
):
    own_rows = hidden_in.astype(jnp.float32)
    q_cols = w_query.shape[1]
    k_cols = w_key.shape[1]
    out_rows = w_output.shape[0]
    width = w_output.shape[1]
    packed = jnp.concatenate(
        [w_query, w_key, value_weight, w_output.reshape(w_query.shape[0], -1)], axis=1
    )
    weights = gathered_over_ctx(packed)
    in_cols = q_cols + 2 * k_cols
    w_in = weights[:, :in_cols]
    ctx_count = weights.shape[0] // w_query.shape[0]
    out_weight = weights[:, in_cols:].reshape(ctx_count * out_rows, width)

    raw_rows = lax.all_gather(hidden_in, HEAD, axis=0, tiled=True)
    normed = root_mean_scale(raw_rows.astype(jnp.float32), pre_gain).astype(jnp.bfloat16)
    tok_count = normed.shape[0]
    projected = jnp.dot(normed, w_in, preferred_element_type=jnp.float32)
    query_raw = projected[:, :q_cols]
    key_unnormed = projected[:, q_cols : q_cols + k_cols]
    value_unnormed = projected[:, q_cols + k_cols :]

    local_heads = q_cols // HEAD_SIZE
    local_groups = k_cols // HEAD_SIZE
    heads_per_group = local_heads // local_groups
    ctx_index = lax.axis_index(CTX)
    token_places = ctx_index * tok_count + jnp.arange(tok_count, dtype=jnp.int32)
    query_matrix = (
        apply_rotary(
            root_mean_scale(query_raw.reshape(tok_count, local_heads, HEAD_SIZE), query_gain),
            token_places,
        )
        * query_scale
    ).astype(jnp.bfloat16)
    projected_keys = apply_rotary(
        root_mean_scale(key_unnormed.reshape(tok_count, local_groups, HEAD_SIZE), key_norm_gain),
        token_places,
    ).astype(jnp.bfloat16)
    projected_values = value_unnormed.astype(jnp.bfloat16)
    key_value = jnp.stack(
        [projected_keys.reshape(tok_count, local_groups * HEAD_SIZE), projected_values]
    )
    pieces = [passed_along(key_value, CTX, 1)]
    extended = jnp.concatenate(pieces + [key_value], axis=1)
    band_keys = extended[0].reshape(-1, local_groups, HEAD_SIZE)
    band_values = extended[1].reshape(-1, local_groups, HEAD_SIZE)
    block_rows = min(512, tok_count)
    grouped_queries = query_matrix.reshape(tok_count, local_groups, heads_per_group, HEAD_SIZE)
    outputs = []
    for block_index in range(tok_count // block_rows):
        first_row = block_index * block_rows
        query_block = grouped_queries[first_row : first_row + block_rows]
        key_block = band_keys[first_row : first_row + block_rows + WINDOW_SPAN]
        value_block = band_values[first_row : first_row + block_rows + WINDOW_SPAN]
        scores = jnp.einsum(
            "qjgd,kjd->jgqk", query_block, key_block, preferred_element_type=jnp.float32
        )
        query_spots = token_places[first_row : first_row + block_rows]
        key_spots = (
            ctx_index * tok_count
            - WINDOW_SPAN
            + first_row
            + jnp.arange(block_rows + WINDOW_SPAN, dtype=jnp.int32)
        )
        allowed = (
            (key_spots[None, :] <= query_spots[:, None])
            & (key_spots[None, :] > query_spots[:, None] - WINDOW_SPAN)
            & (key_spots[None, :] >= 0)
        )
        scores = jnp.where(allowed, scores, mask_value)
        row_max = jnp.max(scores, axis=-1, keepdims=True)
        weights = jnp.exp(scores - row_max)
        row_sum = jnp.sum(weights, axis=-1, keepdims=True)
        probabilities = (weights / row_sum).astype(jnp.bfloat16)
        mixed = jnp.einsum(
            "jgqk,kjd->qjgd", probabilities, value_block, preferred_element_type=jnp.float32
        )
        outputs.append(mixed.astype(jnp.bfloat16).reshape(block_rows, local_heads * HEAD_SIZE))
    attended = jnp.concatenate(outputs, axis=0)

    partial_value = jnp.dot(attended, out_weight, preferred_element_type=jnp.float32).astype(
        jnp.bfloat16
    )
    summed = lax.psum_scatter(
        partial_value, HEAD, scatter_dimension=0, tiled=True
    ).astype(jnp.float32)
    result = own_rows + root_mean_scale(summed, post_gain)
    return result.astype(jnp.bfloat16)


def solution(mesh):
    ctx_size, head_size = mesh.devices.shape
    view = Mesh(
        mesh.devices.reshape(ctx_size // 2, 2, head_size // 2, 2), CTX + HEAD
    )
    rows_spec = P(CTX + HEAD, None)
    cols_spec = P(CTX, HEAD)
    return jax.shard_map(
        body,
        mesh=view,
        in_specs=(
            rows_spec,
            P(),
            cols_spec,
            cols_spec,
            cols_spec,
            P(),
            P(),
            P(HEAD + CTX, None),
            P(),
        ),
        out_specs=rows_spec,
        check_vma=False,
    )
```

```python
import jax
import jax.numpy as jnp
from jax import lax
from jax.sharding import Mesh, PartitionSpec as P

HEAD_SIZE = 128
WINDOW_SPAN = 1024


norm_eps = 1e-06
query_scale = 168.0 ** (-0.5)
rope_base = 10000.0
mask_value = -1e30
CTX = ("cx", "cy")
HEAD = ("hc", "core")


def passed_along(shard, axis, by):
    count = lax.axis_size(axis)
    pairs = [(i, i + by) for i in range(count) if 0 <= i + by < count]
    return lax.ppermute(shard, axis, pairs)


def rotated(shard, axis, by):
    count = lax.axis_size(axis)
    pairs = [(i, (i + by) % count) for i in range(count)]
    return lax.ppermute(shard, axis, pairs)


def placed(parts, me, count):
    stacked = jnp.zeros((count,) + parts[0].shape, parts[0].dtype)
    for i, part in enumerate(parts):
        stacked = lax.dynamic_update_index_in_dim(stacked, part, (me + i) % count, 0)
    return stacked


def ring_over_cx(piece):
    half = piece.shape[0] // 2
    from_left = rotated(piece, "cx", 1)
    from_right = rotated(piece, "cx", -1)
    far = jnp.concatenate(
        [rotated(from_left[:half], "cx", 1), rotated(from_right[half:], "cx", -1)]
    )
    return [piece, from_right, far, from_left]


def gathered_over_ctx(piece):
    cy = lax.axis_index("cy")
    cx = lax.axis_index("cx")
    own = ring_over_cx(piece)
    partner = ring_over_cx(rotated(piece, "cy", 1))
    pairs = [placed([a, b], cy, 2) for a, b in zip(own, partner)]
    ring = placed(pairs, cx, 4)
    return ring.reshape((8 * piece.shape[0],) + piece.shape[1:])


def root_mean_scale(values, scaling):
    mean_sq = jnp.mean(values * values, axis=-1, keepdims=True)
    return values * lax.rsqrt(mean_sq + norm_eps) * scaling


def apply_rotary(values, token_places):
    full_width = values.shape[-1]
    half_width = full_width // 2
    frequency = rope_base ** (-jnp.arange(half_width, dtype=jnp.float32) * 2.0 / full_width)
    angles = token_places.astype(jnp.float32)[:, None] * frequency[None, :]
    cosine = jnp.cos(angles)[:, None, :]
    sine_part = jnp.sin(angles)[:, None, :]
    lower_half = values[..., :half_width]
    upper_half = values[..., half_width:]
    return jnp.concatenate(
        [
            lower_half * cosine - upper_half * sine_part,
            upper_half * cosine + lower_half * sine_part,
        ],
        axis=-1,
    )


def body(
    hidden_in,
    pre_gain,
    w_query,
    w_key,
    value_weight,
    query_gain,
    key_norm_gain,
    w_output,
    post_gain,
):
    own_rows = hidden_in.astype(jnp.float32)
    q_cols = w_query.shape[1]
    k_cols = w_key.shape[1]
    w_in = gathered_over_ctx(jnp.concatenate([w_query, w_key, value_weight], axis=1))

    own_normed = root_mean_scale(own_rows, pre_gain).astype(jnp.bfloat16)
    normed = lax.all_gather(own_normed, HEAD, axis=0, tiled=True)
    tok_count = normed.shape[0]
    projected = jnp.dot(normed, w_in, preferred_element_type=jnp.float32)
    projected, w_output = lax.optimization_barrier((projected, w_output))
    out_weight = gathered_over_ctx(w_output)
    query_raw = projected[:, :q_cols]
    key_unnormed = projected[:, q_cols : q_cols + k_cols]
    value_unnormed = projected[:, q_cols + k_cols :]

    local_heads = q_cols // HEAD_SIZE
    local_groups = k_cols // HEAD_SIZE
    heads_per_group = local_heads // local_groups
    ctx_index = lax.axis_index(CTX)
    token_places = ctx_index * tok_count + jnp.arange(tok_count, dtype=jnp.int32)
    query_matrix = (
        apply_rotary(
            root_mean_scale(query_raw.reshape(tok_count, local_heads, HEAD_SIZE), query_gain),
            token_places,
        )
        * query_scale
    ).astype(jnp.bfloat16)
    projected_keys = apply_rotary(
        root_mean_scale(key_unnormed.reshape(tok_count, local_groups, HEAD_SIZE), key_norm_gain),
        token_places,
    ).astype(jnp.bfloat16)
    projected_values = value_unnormed.astype(jnp.bfloat16)
    key_value = jnp.stack(
        [projected_keys.reshape(tok_count, local_groups * HEAD_SIZE), projected_values]
    )
    pieces = [passed_along(key_value, CTX, 1)]
    extended = jnp.concatenate(pieces + [key_value], axis=1)
    band_keys = extended[0].reshape(-1, local_groups, HEAD_SIZE)
    band_values = extended[1].reshape(-1, local_groups, HEAD_SIZE)
    block_rows = min(512, tok_count)
    grouped_queries = query_matrix.reshape(tok_count, local_groups, heads_per_group, HEAD_SIZE)
    outputs = []
    for block_index in range(tok_count // block_rows):
        first_row = block_index * block_rows
        query_block = grouped_queries[first_row : first_row + block_rows]
        key_block = band_keys[first_row : first_row + block_rows + WINDOW_SPAN]
        value_block = band_values[first_row : first_row + block_rows + WINDOW_SPAN]
        scores = jnp.einsum(
            "qjgd,kjd->jgqk", query_block, key_block, preferred_element_type=jnp.float32
        )
        query_spots = token_places[first_row : first_row + block_rows]
        key_spots = (
            ctx_index * tok_count
            - WINDOW_SPAN
            + first_row
            + jnp.arange(block_rows + WINDOW_SPAN, dtype=jnp.int32)
        )
        allowed = (
            (key_spots[None, :] <= query_spots[:, None])
            & (key_spots[None, :] > query_spots[:, None] - WINDOW_SPAN)
            & (key_spots[None, :] >= 0)
        )
        scores = jnp.where(allowed, scores, mask_value)
        row_max = jnp.max(scores, axis=-1, keepdims=True)
        weights = jnp.exp(scores - row_max)
        row_sum = jnp.sum(weights, axis=-1, keepdims=True)
        probabilities = (weights / row_sum).astype(jnp.bfloat16)
        mixed = jnp.einsum(
            "jgqk,kjd->qjgd", probabilities, value_block, preferred_element_type=jnp.float32
        )
        outputs.append(mixed.astype(jnp.bfloat16).reshape(block_rows, local_heads * HEAD_SIZE))
    attended = jnp.concatenate(outputs, axis=0)

    partial_value = jnp.dot(attended, out_weight, preferred_element_type=jnp.float32).astype(
        jnp.bfloat16
    )
    summed = lax.psum_scatter(
        partial_value, HEAD, scatter_dimension=0, tiled=True
    ).astype(jnp.float32)
    result = own_rows + root_mean_scale(summed, post_gain)
    return result.astype(jnp.bfloat16)


def solution(mesh):
    ctx_size, head_size = mesh.devices.shape
    view = Mesh(
        mesh.devices.reshape(ctx_size // 2, 2, head_size // 2, 2), CTX + HEAD
    )
    rows_spec = P(CTX + HEAD, None)
    cols_spec = P(CTX, HEAD)
    return jax.shard_map(
        body,
        mesh=view,
        in_specs=(
            rows_spec,
            P(),
            cols_spec,
            cols_spec,
            cols_spec,
            P(),
            P(),
            P(HEAD + CTX, None),
            P(),
        ),
        out_specs=rows_spec,
        check_vma=False,
    )
```

```python
import jax
import jax.numpy as jnp
from jax import lax
from jax.sharding import Mesh, PartitionSpec as P

HEAD_SIZE = 128
WINDOW_SPAN = 1024


norm_eps = 1e-06
query_scale = 168.0 ** (-0.5)
rope_base = 10000.0
mask_value = -1e30
CTX = ("cx", "cy")
HEAD = ("ylo", "z", "core")
SC_COLUMNS = 3328


def passed_along(shard, axis, by):
    count = lax.axis_size(axis)
    pairs = [(i, i + by) for i in range(count) if 0 <= i + by < count]
    return lax.ppermute(shard, axis, pairs)


def rotated(shard, axis, by):
    count = lax.axis_size(axis)
    pairs = [(i, (i + by) % count) for i in range(count)]
    return lax.ppermute(shard, axis, pairs)


def placed(parts, me, count):
    stacked = jnp.zeros((count,) + parts[0].shape, parts[0].dtype)
    for i, part in enumerate(parts):
        stacked = lax.dynamic_update_index_in_dim(stacked, part, (me + i) % count, 0)
    return stacked


def ring_over_cx(piece):
    half = piece.shape[0] // 2
    from_left = rotated(piece, "cx", 1)
    from_right = rotated(piece, "cx", -1)
    far = jnp.concatenate(
        [rotated(from_left[:half], "cx", 1), rotated(from_right[half:], "cx", -1)]
    )
    return [piece, from_right, far, from_left]


def gathered_over_ctx(piece):
    cy = lax.axis_index("cy")
    cx = lax.axis_index("cx")
    own = ring_over_cx(piece)
    partner = ring_over_cx(rotated(piece, "cy", 1))
    pairs = [placed([a, b], cy, 2) for a, b in zip(own, partner)]
    ring = placed(pairs, cx, 4)
    return ring.reshape((8 * piece.shape[0],) + piece.shape[1:])


def ring_reduced(pair, z_len):
    z = lax.axis_index("z")
    width = pair.shape[-1]
    half = width // 2
    sums = []
    for direction, cols in ((1, slice(0, half)), (-1, slice(half, width))):
        part = pair[..., cols]
        acc = None
        for step in range(z_len - 1):
            chunk = (z - direction * (step + 1)) % z_len
            mine = lax.dynamic_index_in_dim(part, chunk, 1, keepdims=False).astype(jnp.float32)
            if acc is not None:
                mine = mine + acc
            acc = rotated(mine.astype(jnp.bfloat16), "z", direction).astype(jnp.float32)
        sums.append(lax.dynamic_index_in_dim(part, z, 1, keepdims=False).astype(jnp.float32) + acc)
    return jnp.concatenate(sums, axis=-1)


def reduced_by_permutes(attended, weight):
    core = lax.axis_index("core")
    z_len = lax.axis_size("z")
    rows = attended.shape[0] // (2 * z_len * 2)
    blocks = attended.reshape(2, z_len, 2, rows, attended.shape[-1])
    by_core = [
        jnp.dot(
            blocks[:, :, c].reshape(-1, attended.shape[-1]), weight,
            preferred_element_type=jnp.float32,
        ).astype(jnp.bfloat16)
        for c in range(2)
    ]
    give = jnp.where(core == 0, by_core[1], by_core[0])
    keep = jnp.where(core == 0, by_core[0], by_core[1])
    pair = keep.astype(jnp.float32) + rotated(give, "core", 1).astype(jnp.float32)
    pair = pair.astype(jnp.bfloat16).reshape(2, z_len, rows, weight.shape[-1])
    by_plane = ring_reduced(pair, z_len)
    y = lax.axis_index("ylo")
    give = lax.dynamic_index_in_dim(by_plane, 1 - y, 0, keepdims=False)
    keep = lax.dynamic_index_in_dim(by_plane, y, 0, keepdims=False)
    return keep + rotated(give.astype(jnp.bfloat16), "ylo", 1).astype(jnp.float32)


def root_mean_scale(values, scaling):
    mean_sq = jnp.mean(values * values, axis=-1, keepdims=True)
    return values * lax.rsqrt(mean_sq + norm_eps) * scaling


def apply_rotary(values, token_places):
    full_width = values.shape[-1]
    half_width = full_width // 2
    frequency = rope_base ** (-jnp.arange(half_width, dtype=jnp.float32) * 2.0 / full_width)
    angles = token_places.astype(jnp.float32)[:, None] * frequency[None, :]
    cosine = jnp.cos(angles)[:, None, :]
    sine_part = jnp.sin(angles)[:, None, :]
    lower_half = values[..., :half_width]
    upper_half = values[..., half_width:]
    return jnp.concatenate(
        [
            lower_half * cosine - upper_half * sine_part,
            upper_half * cosine + lower_half * sine_part,
        ],
        axis=-1,
    )


def body(
    hidden_in,
    pre_gain,
    w_query,
    w_key,
    value_weight,
    query_gain,
    key_norm_gain,
    w_output,
    post_gain,
):
    own_rows = hidden_in.astype(jnp.float32)
    q_cols = w_query.shape[1]
    k_cols = w_key.shape[1]
    w_in = gathered_over_ctx(jnp.concatenate([w_query, w_key, value_weight], axis=1))

    raw_rows = lax.all_gather(hidden_in, HEAD, axis=0, tiled=True)
    normed = root_mean_scale(raw_rows.astype(jnp.float32), pre_gain).astype(jnp.bfloat16)
    tok_count = normed.shape[0]
    projected = jnp.dot(normed, w_in, preferred_element_type=jnp.float32)
    projected, w_output = lax.optimization_barrier((projected, w_output))
    out_weight = gathered_over_ctx(w_output)
    query_raw = projected[:, :q_cols]
    key_unnormed = projected[:, q_cols : q_cols + k_cols]
    value_unnormed = projected[:, q_cols + k_cols :]

    local_heads = q_cols // HEAD_SIZE
    local_groups = k_cols // HEAD_SIZE
    heads_per_group = local_heads // local_groups
    ctx_index = lax.axis_index(CTX)
    token_places = ctx_index * tok_count + jnp.arange(tok_count, dtype=jnp.int32)
    query_matrix = (
        apply_rotary(
            root_mean_scale(query_raw.reshape(tok_count, local_heads, HEAD_SIZE), query_gain),
            token_places,
        )
        * query_scale
    ).astype(jnp.bfloat16)
    projected_keys = apply_rotary(
        root_mean_scale(key_unnormed.reshape(tok_count, local_groups, HEAD_SIZE), key_norm_gain),
        token_places,
    ).astype(jnp.bfloat16)
    projected_values = value_unnormed.astype(jnp.bfloat16)
    key_value = jnp.stack(
        [projected_keys.reshape(tok_count, local_groups * HEAD_SIZE), projected_values]
    )
    pieces = [passed_along(key_value, CTX, 1)]
    extended = jnp.concatenate(pieces + [key_value], axis=1)
    band_keys = extended[0].reshape(-1, local_groups, HEAD_SIZE)
    band_values = extended[1].reshape(-1, local_groups, HEAD_SIZE)
    block_rows = min(512, tok_count)
    grouped_queries = query_matrix.reshape(tok_count, local_groups, heads_per_group, HEAD_SIZE)
    outputs = []
    for block_index in range(tok_count // block_rows):
        first_row = block_index * block_rows
        query_block = grouped_queries[first_row : first_row + block_rows]
        key_block = band_keys[first_row : first_row + block_rows + WINDOW_SPAN]
        value_block = band_values[first_row : first_row + block_rows + WINDOW_SPAN]
        scores = jnp.einsum(
            "qjgd,kjd->jgqk", query_block, key_block, preferred_element_type=jnp.float32
        )
        query_spots = token_places[first_row : first_row + block_rows]
        key_spots = (
            ctx_index * tok_count
            - WINDOW_SPAN
            + first_row
            + jnp.arange(block_rows + WINDOW_SPAN, dtype=jnp.int32)
        )
        allowed = (
            (key_spots[None, :] <= query_spots[:, None])
            & (key_spots[None, :] > query_spots[:, None] - WINDOW_SPAN)
            & (key_spots[None, :] >= 0)
        )
        scores = jnp.where(allowed, scores, mask_value)
        row_max = jnp.max(scores, axis=-1, keepdims=True)
        weights = jnp.exp(scores - row_max)
        row_sum = jnp.sum(weights, axis=-1, keepdims=True)
        probabilities = (weights / row_sum).astype(jnp.bfloat16)
        mixed = jnp.einsum(
            "jgqk,kjd->qjgd", probabilities, value_block, preferred_element_type=jnp.float32
        )
        outputs.append(mixed.astype(jnp.bfloat16).reshape(block_rows, local_heads * HEAD_SIZE))
    attended = jnp.concatenate(outputs, axis=0)

    split = SC_COLUMNS
    partial_value = jnp.dot(
        attended, out_weight[:, :split], preferred_element_type=jnp.float32
    ).astype(jnp.bfloat16)
    summed = jnp.concatenate(
        [
            lax.psum_scatter(partial_value, HEAD, scatter_dimension=0, tiled=True).astype(
                jnp.float32
            ),
            reduced_by_permutes(attended, out_weight[:, split:]),
        ],
        axis=-1,
    )
    result = own_rows + root_mean_scale(summed, post_gain)
    return result.astype(jnp.bfloat16)


def solution(mesh):
    ctx_size, head_size = mesh.devices.shape
    view = Mesh(
        mesh.devices.reshape(ctx_size // 2, 2, 2, head_size // 4, 2), CTX + HEAD
    )
    rows_spec = P(CTX + HEAD, None)
    cols_spec = P(CTX, HEAD)
    return jax.shard_map(
        body,
        mesh=view,
        in_specs=(
            rows_spec,
            P(),
            cols_spec,
            cols_spec,
            cols_spec,
            P(),
            P(),
            P(HEAD + CTX, None),
            P(),
        ),
        out_specs=rows_spec,
        check_vma=False,
    )
```

```python
import jax
import jax.numpy as jnp
from jax import lax
from jax.sharding import Mesh, PartitionSpec as P

HEAD_SIZE = 128
WINDOW_SPAN = 1024


norm_eps = 1e-06
query_scale = 168.0 ** (-0.5)
rope_base = 10000.0
mask_value = -1e30
CTX = ("cx", "cy")
HEAD = ("hc", "core")


def passed_along(shard, axis, by):
    count = lax.axis_size(axis)
    pairs = [(i, i + by) for i in range(count) if 0 <= i + by < count]
    return lax.ppermute(shard, axis, pairs)


def rotated(shard, axis, by):
    count = lax.axis_size(axis)
    pairs = [(i, (i + by) % count) for i in range(count)]
    return lax.ppermute(shard, axis, pairs)


def placed(parts, me, count):
    stacked = jnp.zeros((count,) + parts[0].shape, parts[0].dtype)
    for i, part in enumerate(parts):
        stacked = lax.dynamic_update_index_in_dim(stacked, part, (me + i) % count, 0)
    return stacked


def ring_over_cx(piece):
    half = piece.shape[0] // 2
    from_left = rotated(piece, "cx", 1)
    from_right = rotated(piece, "cx", -1)
    far = jnp.concatenate(
        [rotated(from_left[:half], "cx", 1), rotated(from_right[half:], "cx", -1)]
    )
    return [piece, from_right, far, from_left]


def gathered_over_ctx(piece):
    cy = lax.axis_index("cy")
    cx = lax.axis_index("cx")
    own = ring_over_cx(piece)
    partner = ring_over_cx(rotated(piece, "cy", 1))
    pairs = [placed([a, b], cy, 2) for a, b in zip(own, partner)]
    ring = placed(pairs, cx, 4)
    return ring.reshape((8 * piece.shape[0],) + piece.shape[1:])


def root_mean_scale(values, scaling):
    mean_sq = jnp.mean(values * values, axis=-1, keepdims=True)
    return values * lax.rsqrt(mean_sq + norm_eps) * scaling


def apply_rotary(values, token_places):
    full_width = values.shape[-1]
    half_width = full_width // 2
    frequency = rope_base ** (-jnp.arange(half_width, dtype=jnp.float32) * 2.0 / full_width)
    angles = token_places.astype(jnp.float32)[:, None] * frequency[None, :]
    cosine = jnp.cos(angles)[:, None, :]
    sine_part = jnp.sin(angles)[:, None, :]
    lower_half = values[..., :half_width]
    upper_half = values[..., half_width:]
    return jnp.concatenate(
        [
            lower_half * cosine - upper_half * sine_part,
            upper_half * cosine + lower_half * sine_part,
        ],
        axis=-1,
    )


def body(
    hidden_in,
    pre_gain,
    w_query,
    w_key,
    value_weight,
    query_gain,
    key_norm_gain,
    w_output,
    post_gain,
):
    own_rows = hidden_in.astype(jnp.float32)
    q_cols = w_query.shape[1]
    k_cols = w_key.shape[1]
    w_in = gathered_over_ctx(jnp.concatenate([w_query, w_key, value_weight], axis=1))

    own_normed = root_mean_scale(own_rows, pre_gain).astype(jnp.bfloat16)
    normed = lax.all_gather(own_normed, HEAD, axis=0, tiled=True)
    normed, w_output = lax.optimization_barrier((normed, w_output))
    out_weight = gathered_over_ctx(w_output)
    tok_count = normed.shape[0]
    projected = jnp.dot(normed, w_in, preferred_element_type=jnp.float32)
    query_raw = projected[:, :q_cols]
    key_unnormed = projected[:, q_cols : q_cols + k_cols]
    value_unnormed = projected[:, q_cols + k_cols :]

    local_heads = q_cols // HEAD_SIZE
    local_groups = k_cols // HEAD_SIZE
    heads_per_group = local_heads // local_groups
    ctx_index = lax.axis_index(CTX)
    token_places = ctx_index * tok_count + jnp.arange(tok_count, dtype=jnp.int32)
    query_matrix = (
        apply_rotary(
            root_mean_scale(query_raw.reshape(tok_count, local_heads, HEAD_SIZE), query_gain),
            token_places,
        )
        * query_scale
    ).astype(jnp.bfloat16)
    projected_keys = apply_rotary(
        root_mean_scale(key_unnormed.reshape(tok_count, local_groups, HEAD_SIZE), key_norm_gain),
        token_places,
    ).astype(jnp.bfloat16)
    projected_values = value_unnormed.astype(jnp.bfloat16)
    key_value = jnp.stack(
        [projected_keys.reshape(tok_count, local_groups * HEAD_SIZE), projected_values]
    )
    pieces = [passed_along(key_value, CTX, 1)]
    extended = jnp.concatenate(pieces + [key_value], axis=1)
    band_keys = extended[0].reshape(-1, local_groups, HEAD_SIZE)
    band_values = extended[1].reshape(-1, local_groups, HEAD_SIZE)
    block_rows = min(512, tok_count)
    grouped_queries = query_matrix.reshape(tok_count, local_groups, heads_per_group, HEAD_SIZE)
    outputs = []
    for block_index in range(tok_count // block_rows):
        first_row = block_index * block_rows
        query_block = grouped_queries[first_row : first_row + block_rows]
        key_block = band_keys[first_row : first_row + block_rows + WINDOW_SPAN]
        value_block = band_values[first_row : first_row + block_rows + WINDOW_SPAN]
        scores = jnp.einsum(
            "qjgd,kjd->jgqk", query_block, key_block, preferred_element_type=jnp.float32
        )
        query_spots = token_places[first_row : first_row + block_rows]
        key_spots = (
            ctx_index * tok_count
            - WINDOW_SPAN
            + first_row
            + jnp.arange(block_rows + WINDOW_SPAN, dtype=jnp.int32)
        )
        allowed = (
            (key_spots[None, :] <= query_spots[:, None])
            & (key_spots[None, :] > query_spots[:, None] - WINDOW_SPAN)
            & (key_spots[None, :] >= 0)
        )
        scores = jnp.where(allowed, scores, mask_value)
        row_max = jnp.max(scores, axis=-1, keepdims=True)
        weights = jnp.exp(scores - row_max)
        row_sum = jnp.sum(weights, axis=-1, keepdims=True)
        probabilities = (weights / row_sum).astype(jnp.bfloat16)
        mixed = jnp.einsum(
            "jgqk,kjd->qjgd", probabilities, value_block, preferred_element_type=jnp.float32
        )
        outputs.append(mixed.astype(jnp.bfloat16).reshape(block_rows, local_heads * HEAD_SIZE))
    attended = jnp.concatenate(outputs, axis=0)

    partial_value = jnp.dot(attended, out_weight, preferred_element_type=jnp.float32).astype(
        jnp.bfloat16
    )
    summed = lax.psum_scatter(
        partial_value, HEAD, scatter_dimension=0, tiled=True
    ).astype(jnp.float32)
    result = own_rows + root_mean_scale(summed, post_gain)
    return result.astype(jnp.bfloat16)


def solution(mesh):
    ctx_size, head_size = mesh.devices.shape
    view = Mesh(
        mesh.devices.reshape(ctx_size // 2, 2, head_size // 2, 2), CTX + HEAD
    )
    rows_spec = P(CTX + HEAD, None)
    cols_spec = P(CTX, HEAD)
    return jax.shard_map(
        body,
        mesh=view,
        in_specs=(
            rows_spec,
            P(),
            cols_spec,
            cols_spec,
            cols_spec,
            P(),
            P(),
            P(HEAD + CTX, None),
            P(),
        ),
        out_specs=rows_spec,
        check_vma=False,
    )
```

```python
import jax
import jax.numpy as jnp
from jax import lax
from jax.sharding import Mesh, PartitionSpec as P


HEAD_SIZE = 128
WINDOW_SPAN = 1024


norm_eps = 1e-06
query_scale = 168.0 ** (-0.5)
rope_base = 10000.0
mask_value = -1e30
CTX = ("cx", "cy")
HEAD = ("hc", "core")


def passed_along(shard, axis, by):
    count = lax.axis_size(axis)
    pairs = [(i, i + by) for i in range(count) if 0 <= i + by < count]
    return lax.ppermute(shard, axis, pairs)


def rotated(shard, axis, by):
    count = lax.axis_size(axis)
    pairs = [(i, (i + by) % count) for i in range(count)]
    return lax.ppermute(shard, axis, pairs)


def placed(parts, me, count):
    stacked = jnp.zeros((count,) + parts[0].shape, parts[0].dtype)
    for i, part in enumerate(parts):
        stacked = lax.dynamic_update_index_in_dim(stacked, part, (me + i) % count, 0)
    return stacked


def ring_over_cx(piece):
    half = piece.shape[0] // 2
    from_left = rotated(piece, "cx", 1)
    from_right = rotated(piece, "cx", -1)
    far = jnp.concatenate(
        [rotated(from_left[:half], "cx", 1), rotated(from_right[half:], "cx", -1)]
    )
    return [piece, from_right, far, from_left]


def gathered_over_ctx(piece):
    cy = lax.axis_index("cy")
    cx = lax.axis_index("cx")
    own = ring_over_cx(piece)
    crossed = rotated(piece, "cy", 1)
    partner = ring_over_cx(crossed)
    pairs = [placed([a, b], cy, 2) for a, b in zip(own, partner)]
    ring = placed(pairs, cx, 4)
    return ring.reshape((8 * piece.shape[0],) + piece.shape[1:])


def root_mean_scale(values, scaling):
    mean_sq = jnp.mean(values * values, axis=-1, keepdims=True)
    return values * lax.rsqrt(mean_sq + norm_eps) * scaling


def apply_rotary(values, token_places):
    full_width = values.shape[-1]
    half_width = full_width // 2
    frequency = rope_base ** (-jnp.arange(half_width, dtype=jnp.float32) * 2.0 / full_width)
    angles = token_places.astype(jnp.float32)[:, None] * frequency[None, :]
    cosine = jnp.cos(angles)[:, None, :]
    sine_part = jnp.sin(angles)[:, None, :]
    lower_half = values[..., :half_width]
    upper_half = values[..., half_width:]
    return jnp.concatenate(
        [
            lower_half * cosine - upper_half * sine_part,
            upper_half * cosine + lower_half * sine_part,
        ],
        axis=-1,
    )


def layer(
    hidden_in,
    pre_gain,
    w_query,
    w_key,
    value_weight,
    query_gain,
    key_norm_gain,
    w_output,
    post_gain,
):
    own_rows = hidden_in.astype(jnp.float32)
    q_cols = w_query.shape[1]
    k_cols = w_key.shape[1]
    w_in = gathered_over_ctx(jnp.concatenate([w_query, w_key, value_weight], axis=1))

    own_normed = root_mean_scale(own_rows, pre_gain).astype(jnp.bfloat16)
    normed = lax.all_gather(own_normed, HEAD, axis=0, tiled=True)
    normed, w_output = lax.optimization_barrier((normed, w_output))
    out_weight = gathered_over_ctx(w_output)
    tok_count = normed.shape[0]
    projected = jnp.dot(normed, w_in, preferred_element_type=jnp.float32)
    query_raw = projected[:, :q_cols]
    key_unnormed = projected[:, q_cols : q_cols + k_cols]
    value_unnormed = projected[:, q_cols + k_cols :]

    local_heads = q_cols // HEAD_SIZE
    local_groups = k_cols // HEAD_SIZE
    heads_per_group = local_heads // local_groups
    ctx_index = lax.axis_index(CTX)
    token_places = ctx_index * tok_count + jnp.arange(tok_count, dtype=jnp.int32)
    query_matrix = (
        apply_rotary(
            root_mean_scale(query_raw.reshape(tok_count, local_heads, HEAD_SIZE), query_gain),
            token_places,
        )
        * query_scale
    ).astype(jnp.bfloat16)
    projected_keys = apply_rotary(
        root_mean_scale(key_unnormed.reshape(tok_count, local_groups, HEAD_SIZE), key_norm_gain),
        token_places,
    ).astype(jnp.bfloat16)
    projected_values = value_unnormed.astype(jnp.bfloat16)
    key_value = jnp.stack(
        [projected_keys.reshape(tok_count, local_groups * HEAD_SIZE), projected_values]
    )
    pieces = [passed_along(key_value, CTX, 1)]
    extended = jnp.concatenate(pieces + [key_value], axis=1)
    band_keys = extended[0].reshape(-1, local_groups, HEAD_SIZE)
    band_values = extended[1].reshape(-1, local_groups, HEAD_SIZE)
    block_rows = min(512, tok_count)
    grouped_queries = query_matrix.reshape(tok_count, local_groups, heads_per_group, HEAD_SIZE)
    outputs = []
    for block_index in range(tok_count // block_rows):
        first_row = block_index * block_rows
        query_block = grouped_queries[first_row : first_row + block_rows]
        key_block = band_keys[first_row : first_row + block_rows + WINDOW_SPAN]
        value_block = band_values[first_row : first_row + block_rows + WINDOW_SPAN]
        scores = jnp.einsum(
            "qjgd,kjd->jgqk", query_block, key_block, preferred_element_type=jnp.float32
        )
        query_spots = token_places[first_row : first_row + block_rows]
        key_spots = (
            ctx_index * tok_count
            - WINDOW_SPAN
            + first_row
            + jnp.arange(block_rows + WINDOW_SPAN, dtype=jnp.int32)
        )
        allowed = (
            (key_spots[None, :] <= query_spots[:, None])
            & (key_spots[None, :] > query_spots[:, None] - WINDOW_SPAN)
            & (key_spots[None, :] >= 0)
        )
        scores = jnp.where(allowed, scores, mask_value)
        row_max = jnp.max(scores, axis=-1, keepdims=True)
        weights = jnp.exp(scores - row_max)
        row_sum = jnp.sum(weights, axis=-1, keepdims=True)
        probabilities = (weights / row_sum).astype(jnp.bfloat16)
        mixed = jnp.einsum(
            "jgqk,kjd->qjgd", probabilities, value_block, preferred_element_type=jnp.float32
        )
        outputs.append(mixed.astype(jnp.bfloat16).reshape(block_rows, local_heads * HEAD_SIZE))
    attended = jnp.concatenate(outputs, axis=0)

    partial_value = jnp.dot(attended, out_weight, preferred_element_type=jnp.float32).astype(
        jnp.bfloat16
    )
    summed = lax.psum_scatter(
        partial_value, HEAD, scatter_dimension=0, tiled=True
    ).astype(jnp.float32)
    result = own_rows + root_mean_scale(summed, post_gain)
    return result.astype(jnp.bfloat16)


def solution(mesh):
    ctx_size, head_size = mesh.devices.shape
    view = Mesh(
        mesh.devices.reshape(ctx_size // 2, 2, head_size // 2, 2), CTX + HEAD
    )
    rows_spec = P(CTX + HEAD, None)
    cols_spec = P(CTX, HEAD)
    return jax.shard_map(
        layer,
        mesh=view,
        in_specs=(
            rows_spec,
            P(),
            cols_spec,
            cols_spec,
            cols_spec,
            P(),
            P(),
            P(HEAD + CTX, None),
            P(),
        ),
        out_specs=rows_spec,
        check_vma=False,
    )
```

```python
import jax
import jax.numpy as jnp
from jax import lax
from jax.sharding import Mesh, PartitionSpec as P

HEAD_SIZE = 128
WINDOW_SPAN = 1024


norm_eps = 1e-06
query_scale = 168.0 ** (-0.5)
rope_base = 10000.0
mask_value = -1e30
CTX = ("cx", "cy")
HEAD = ("hc", "core")


def passed_along(shard, axis, by):
    count = lax.axis_size(axis)
    pairs = [(i, i + by) for i in range(count) if 0 <= i + by < count]
    return lax.ppermute(shard, axis, pairs)


def rotated(shard, axis, by):
    count = lax.axis_size(axis)
    pairs = [(i, (i + by) % count) for i in range(count)]
    return lax.ppermute(shard, axis, pairs)


def placed(parts, me, count):
    stacked = jnp.zeros((count,) + parts[0].shape, parts[0].dtype)
    for i, part in enumerate(parts):
        stacked = lax.dynamic_update_index_in_dim(stacked, part, (me + i) % count, 0)
    return stacked


def ring_over_cx(piece):
    half = piece.shape[0] // 2
    from_left = rotated(piece, "cx", 1)
    from_right = rotated(piece, "cx", -1)
    far = jnp.concatenate(
        [rotated(from_left[:half], "cx", 1), rotated(from_right[half:], "cx", -1)]
    )
    return [piece, from_right, far, from_left]


def gathered_over_ctx(piece):
    cy = lax.axis_index("cy")
    cx = lax.axis_index("cx")
    own = ring_over_cx(piece)
    partner = ring_over_cx(rotated(piece, "cy", 1))
    pairs = [placed([a, b], cy, 2) for a, b in zip(own, partner)]
    ring = placed(pairs, cx, 4)
    return ring.reshape((8 * piece.shape[0],) + piece.shape[1:])


def root_mean_scale(values, scaling):
    mean_sq = jnp.mean(values * values, axis=-1, keepdims=True)
    return values * lax.rsqrt(mean_sq + norm_eps) * scaling


def apply_rotary(values, token_places):
    full_width = values.shape[-1]
    half_width = full_width // 2
    frequency = rope_base ** (-jnp.arange(half_width, dtype=jnp.float32) * 2.0 / full_width)
    angles = token_places.astype(jnp.float32)[:, None] * frequency[None, :]
    cosine = jnp.cos(angles)[:, None, :]
    sine_part = jnp.sin(angles)[:, None, :]
    lower_half = values[..., :half_width]
    upper_half = values[..., half_width:]
    return jnp.concatenate(
        [
            lower_half * cosine - upper_half * sine_part,
            upper_half * cosine + lower_half * sine_part,
        ],
        axis=-1,
    )


def body(
    hidden_in,
    pre_gain,
    w_query,
    w_key,
    value_weight,
    query_gain,
    key_norm_gain,
    w_output,
    post_gain,
):
    own_rows = hidden_in.astype(jnp.float32)
    q_cols = w_query.shape[1]
    k_cols = w_key.shape[1]
    w_in = gathered_over_ctx(jnp.concatenate([w_query, w_key, value_weight], axis=1))

    own_normed = root_mean_scale(own_rows, pre_gain).astype(jnp.bfloat16)
    normed = lax.all_gather(own_normed, HEAD, axis=0, tiled=True)
    normed, w_output = lax.optimization_barrier((normed, w_output))
    out_weight = gathered_over_ctx(w_output)
    tok_count = normed.shape[0]
    projected = jnp.dot(normed, w_in, preferred_element_type=jnp.float32)
    query_raw = projected[:, :q_cols]
    key_unnormed = projected[:, q_cols : q_cols + k_cols]
    value_unnormed = projected[:, q_cols + k_cols :]

    local_heads = q_cols // HEAD_SIZE
    local_groups = k_cols // HEAD_SIZE
    heads_per_group = local_heads // local_groups
    ctx_index = lax.axis_index(CTX)
    token_places = ctx_index * tok_count + jnp.arange(tok_count, dtype=jnp.int32)
    query_matrix = (
        apply_rotary(
            root_mean_scale(query_raw.reshape(tok_count, local_heads, HEAD_SIZE), query_gain),
            token_places,
        )
        * query_scale
    ).astype(jnp.bfloat16)
    projected_keys = apply_rotary(
        root_mean_scale(key_unnormed.reshape(tok_count, local_groups, HEAD_SIZE), key_norm_gain),
        token_places,
    ).astype(jnp.bfloat16)
    projected_values = value_unnormed.astype(jnp.bfloat16)
    key_value = jnp.stack(
        [projected_keys.reshape(tok_count, local_groups * HEAD_SIZE), projected_values]
    )
    pieces = [passed_along(key_value, CTX, 1)]
    extended = jnp.concatenate(pieces + [key_value], axis=1)
    band_keys = extended[0].reshape(-1, local_groups, HEAD_SIZE)
    band_values = extended[1].reshape(-1, local_groups, HEAD_SIZE)
    block_rows = min(512, tok_count)
    grouped_queries = query_matrix.reshape(tok_count, local_groups, heads_per_group, HEAD_SIZE)
    outputs = []
    for block_index in range(tok_count // block_rows):
        first_row = block_index * block_rows
        query_block = grouped_queries[first_row : first_row + block_rows]
        key_block = band_keys[first_row : first_row + block_rows + WINDOW_SPAN]
        value_block = band_values[first_row : first_row + block_rows + WINDOW_SPAN]
        scores = jnp.einsum(
            "qjgd,kjd->jgqk", query_block, key_block, preferred_element_type=jnp.float32
        )
        query_spots = token_places[first_row : first_row + block_rows]
        key_spots = (
            ctx_index * tok_count
            - WINDOW_SPAN
            + first_row
            + jnp.arange(block_rows + WINDOW_SPAN, dtype=jnp.int32)
        )
        allowed = (
            (key_spots[None, :] <= query_spots[:, None])
            & (key_spots[None, :] > query_spots[:, None] - WINDOW_SPAN)
            & (key_spots[None, :] >= 0)
        )
        scores = jnp.where(allowed, scores, mask_value)
        row_max = jnp.max(scores, axis=-1, keepdims=True)
        weights = jnp.exp(scores - row_max)
        row_sum = jnp.sum(weights, axis=-1, keepdims=True)
        probabilities = (weights / row_sum).astype(jnp.bfloat16)
        mixed = jnp.einsum(
            "jgqk,kjd->qjgd", probabilities, value_block, preferred_element_type=jnp.float32
        )
        outputs.append(mixed.astype(jnp.bfloat16).reshape(block_rows, local_heads * HEAD_SIZE))
    attended = jnp.concatenate(outputs, axis=0)

    core = lax.axis_index("core")
    chips = lax.axis_size("hc")
    rows = tok_count // (2 * chips)
    blocks = attended.reshape(chips, 2, rows, attended.shape[-1])
    by_core = [
        jnp.dot(
            blocks[:, c].reshape(chips * rows, attended.shape[-1]), out_weight,
            preferred_element_type=jnp.float32,
        ).astype(jnp.bfloat16)
        for c in range(2)
    ]
    give = jnp.where(core == 0, by_core[1], by_core[0])
    keep = jnp.where(core == 0, by_core[0], by_core[1])
    pair_sum = (
        keep.astype(jnp.float32) + rotated(give, "core", 1).astype(jnp.float32)
    ).astype(jnp.bfloat16)
    summed = lax.psum_scatter(
        pair_sum, "hc", scatter_dimension=0, tiled=True
    ).astype(jnp.float32)
    result = own_rows + root_mean_scale(summed, post_gain)
    return result.astype(jnp.bfloat16)


def solution(mesh):
    ctx_size, head_size = mesh.devices.shape
    view = Mesh(
        mesh.devices.reshape(ctx_size // 2, 2, head_size // 2, 2), CTX + HEAD
    )
    rows_spec = P(CTX + HEAD, None)
    cols_spec = P(CTX, HEAD)
    return jax.shard_map(
        body,
        mesh=view,
        in_specs=(
            rows_spec,
            P(),
            cols_spec,
            cols_spec,
            cols_spec,
            P(),
            P(),
            P(HEAD + CTX, None),
            P(),
        ),
        out_specs=rows_spec,
        check_vma=False,
    )
```

```python
import jax
import jax.numpy as jnp
from jax import lax
from jax.sharding import Mesh, PartitionSpec as P

HEAD_SIZE = 128
WINDOW_SPAN = 1024


norm_eps = 1e-06
query_scale = 168.0 ** (-0.5)
rope_base = 10000.0
mask_value = -1e30
CTX = ("cx", "cy")
HEAD = ("hc", "core")


def passed_along(shard, axis, by):
    count = lax.axis_size(axis)
    pairs = [(i, i + by) for i in range(count) if 0 <= i + by < count]
    return lax.ppermute(shard, axis, pairs)


def rotated(shard, axis, by):
    count = lax.axis_size(axis)
    pairs = [(i, (i + by) % count) for i in range(count)]
    return lax.ppermute(shard, axis, pairs)


def placed(parts, me, count):
    stacked = jnp.zeros((count,) + parts[0].shape, parts[0].dtype)
    for i, part in enumerate(parts):
        stacked = lax.dynamic_update_index_in_dim(stacked, part, (me + i) % count, 0)
    return stacked


def ring_over_cx(piece):
    half = piece.shape[0] // 2
    from_left = rotated(piece, "cx", 1)
    from_right = rotated(piece, "cx", -1)
    far = jnp.concatenate(
        [rotated(from_left[:half], "cx", 1), rotated(from_right[half:], "cx", -1)]
    )
    return [piece, from_right, far, from_left]


def gathered_over_ctx(piece):
    cy = lax.axis_index("cy")
    cx = lax.axis_index("cx")
    own = ring_over_cx(piece)
    partner = ring_over_cx(rotated(piece, "cy", 1))
    pairs = [placed([a, b], cy, 2) for a, b in zip(own, partner)]
    ring = placed(pairs, cx, 4)
    return ring.reshape((8 * piece.shape[0],) + piece.shape[1:])


def gathered_directly(piece, axis):
    count = lax.axis_size(axis)
    me = lax.axis_index(axis)
    parts = [piece] + [rotated(piece, axis, by) for by in range(count - 1, 0, -1)]
    stacked = placed(parts, me, count)
    return stacked.reshape((count * piece.shape[0],) + piece.shape[1:])


def root_mean_scale(values, scaling):
    mean_sq = jnp.mean(values * values, axis=-1, keepdims=True)
    return values * lax.rsqrt(mean_sq + norm_eps) * scaling


def apply_rotary(values, token_places):
    full_width = values.shape[-1]
    half_width = full_width // 2
    frequency = rope_base ** (-jnp.arange(half_width, dtype=jnp.float32) * 2.0 / full_width)
    angles = token_places.astype(jnp.float32)[:, None] * frequency[None, :]
    cosine = jnp.cos(angles)[:, None, :]
    sine_part = jnp.sin(angles)[:, None, :]
    lower_half = values[..., :half_width]
    upper_half = values[..., half_width:]
    return jnp.concatenate(
        [
            lower_half * cosine - upper_half * sine_part,
            upper_half * cosine + lower_half * sine_part,
        ],
        axis=-1,
    )


def body(
    hidden_in,
    pre_gain,
    w_query,
    w_key,
    value_weight,
    query_gain,
    key_norm_gain,
    w_output,
    post_gain,
):
    own_rows = hidden_in.astype(jnp.float32)
    q_cols = w_query.shape[1]
    k_cols = w_key.shape[1]
    w_in = gathered_over_ctx(jnp.concatenate([w_query, w_key, value_weight], axis=1))

    own_normed = root_mean_scale(own_rows, pre_gain).astype(jnp.bfloat16)
    normed = lax.all_gather(own_normed, HEAD, axis=0, tiled=True)
    normed, w_output = lax.optimization_barrier((normed, w_output))
    out_weight = gathered_directly(w_output, CTX)
    tok_count = normed.shape[0]
    projected = jnp.dot(normed, w_in, preferred_element_type=jnp.float32)
    query_raw = projected[:, :q_cols]
    key_unnormed = projected[:, q_cols : q_cols + k_cols]
    value_unnormed = projected[:, q_cols + k_cols :]

    local_heads = q_cols // HEAD_SIZE
    local_groups = k_cols // HEAD_SIZE
    heads_per_group = local_heads // local_groups
    ctx_index = lax.axis_index(CTX)
    token_places = ctx_index * tok_count + jnp.arange(tok_count, dtype=jnp.int32)
    query_matrix = (
        apply_rotary(
            root_mean_scale(query_raw.reshape(tok_count, local_heads, HEAD_SIZE), query_gain),
            token_places,
        )
        * query_scale
    ).astype(jnp.bfloat16)
    projected_keys = apply_rotary(
        root_mean_scale(key_unnormed.reshape(tok_count, local_groups, HEAD_SIZE), key_norm_gain),
        token_places,
    ).astype(jnp.bfloat16)
    projected_values = value_unnormed.astype(jnp.bfloat16)
    key_value = jnp.stack(
        [projected_keys.reshape(tok_count, local_groups * HEAD_SIZE), projected_values]
    )
    pieces = [passed_along(key_value, CTX, 1)]
    extended = jnp.concatenate(pieces + [key_value], axis=1)
    band_keys = extended[0].reshape(-1, local_groups, HEAD_SIZE)
    band_values = extended[1].reshape(-1, local_groups, HEAD_SIZE)
    block_rows = min(512, tok_count)
    grouped_queries = query_matrix.reshape(tok_count, local_groups, heads_per_group, HEAD_SIZE)
    outputs = []
    for block_index in range(tok_count // block_rows):
        first_row = block_index * block_rows
        query_block = grouped_queries[first_row : first_row + block_rows]
        key_block = band_keys[first_row : first_row + block_rows + WINDOW_SPAN]
        value_block = band_values[first_row : first_row + block_rows + WINDOW_SPAN]
        scores = jnp.einsum(
            "qjgd,kjd->jgqk", query_block, key_block, preferred_element_type=jnp.float32
        )
        query_spots = token_places[first_row : first_row + block_rows]
        key_spots = (
            ctx_index * tok_count
            - WINDOW_SPAN
            + first_row
            + jnp.arange(block_rows + WINDOW_SPAN, dtype=jnp.int32)
        )
        allowed = (
            (key_spots[None, :] <= query_spots[:, None])
            & (key_spots[None, :] > query_spots[:, None] - WINDOW_SPAN)
            & (key_spots[None, :] >= 0)
        )
        scores = jnp.where(allowed, scores, mask_value)
        row_max = jnp.max(scores, axis=-1, keepdims=True)
        weights = jnp.exp(scores - row_max)
        row_sum = jnp.sum(weights, axis=-1, keepdims=True)
        probabilities = (weights / row_sum).astype(jnp.bfloat16)
        mixed = jnp.einsum(
            "jgqk,kjd->qjgd", probabilities, value_block, preferred_element_type=jnp.float32
        )
        outputs.append(mixed.astype(jnp.bfloat16).reshape(block_rows, local_heads * HEAD_SIZE))
    attended = jnp.concatenate(outputs, axis=0)

    partial_value = jnp.dot(attended, out_weight, preferred_element_type=jnp.float32).astype(
        jnp.bfloat16
    )
    summed = lax.psum_scatter(
        partial_value, HEAD, scatter_dimension=0, tiled=True
    ).astype(jnp.float32)
    result = own_rows + root_mean_scale(summed, post_gain)
    return result.astype(jnp.bfloat16)


def solution(mesh):
    ctx_size, head_size = mesh.devices.shape
    view = Mesh(
        mesh.devices.reshape(ctx_size // 2, 2, head_size // 2, 2), CTX + HEAD
    )
    rows_spec = P(CTX + HEAD, None)
    cols_spec = P(CTX, HEAD)
    return jax.shard_map(
        body,
        mesh=view,
        in_specs=(
            rows_spec,
            P(),
            cols_spec,
            cols_spec,
            cols_spec,
            P(),
            P(),
            P(HEAD + CTX, None),
            P(),
        ),
        out_specs=rows_spec,
        check_vma=False,
    )
```

```python
import jax
import jax.numpy as jnp
from jax import lax
from jax.sharding import Mesh, PartitionSpec as P

HEAD_SIZE = 128
WINDOW_SPAN = 1024


norm_eps = 1e-06
query_scale = 168.0 ** (-0.5)
rope_base = 10000.0
mask_value = -1e30
CTX = ("cx", "cy")
HEAD = ("hc", "core")


def passed_along(shard, axis, by):
    count = lax.axis_size(axis)
    pairs = [(i, i + by) for i in range(count) if 0 <= i + by < count]
    return lax.ppermute(shard, axis, pairs)


def rotated(shard, axis, by):
    count = lax.axis_size(axis)
    pairs = [(i, (i + by) % count) for i in range(count)]
    return lax.ppermute(shard, axis, pairs)


def placed(parts, me, count):
    stacked = jnp.zeros((count,) + parts[0].shape, parts[0].dtype)
    for i, part in enumerate(parts):
        stacked = lax.dynamic_update_index_in_dim(stacked, part, (me + i) % count, 0)
    return stacked


def ring_over_cx(piece):
    half = piece.shape[0] // 2
    from_left = rotated(piece, "cx", 1)
    from_right = rotated(piece, "cx", -1)
    far = jnp.concatenate(
        [rotated(from_left[:half], "cx", 1), rotated(from_right[half:], "cx", -1)]
    )
    return [piece, from_right, far, from_left]


def gathered_over_ctx(piece):
    cy = lax.axis_index("cy")
    cx = lax.axis_index("cx")
    own = ring_over_cx(piece)
    partner = ring_over_cx(rotated(piece, "cy", 1))
    pairs = [placed([a, b], cy, 2) for a, b in zip(own, partner)]
    ring = placed(pairs, cx, 4)
    return ring.reshape((8 * piece.shape[0],) + piece.shape[1:])


def gathered_pair_first(piece):
    cy = lax.axis_index("cy")
    cx = lax.axis_index("cx")
    pair = placed([piece, rotated(piece, "cy", 1)], cy, 2)
    ring = placed(ring_over_cx(pair), cx, 4)
    return ring.reshape((8 * piece.shape[0],) + piece.shape[1:])


def root_mean_scale(values, scaling):
    mean_sq = jnp.mean(values * values, axis=-1, keepdims=True)
    return values * lax.rsqrt(mean_sq + norm_eps) * scaling


def apply_rotary(values, token_places):
    full_width = values.shape[-1]
    half_width = full_width // 2
    frequency = rope_base ** (-jnp.arange(half_width, dtype=jnp.float32) * 2.0 / full_width)
    angles = token_places.astype(jnp.float32)[:, None] * frequency[None, :]
    cosine = jnp.cos(angles)[:, None, :]
    sine_part = jnp.sin(angles)[:, None, :]
    lower_half = values[..., :half_width]
    upper_half = values[..., half_width:]
    return jnp.concatenate(
        [
            lower_half * cosine - upper_half * sine_part,
            upper_half * cosine + lower_half * sine_part,
        ],
        axis=-1,
    )


def body(
    hidden_in,
    pre_gain,
    w_query,
    w_key,
    value_weight,
    query_gain,
    key_norm_gain,
    w_output,
    post_gain,
):
    own_rows = hidden_in.astype(jnp.float32)
    q_cols = w_query.shape[1]
    k_cols = w_key.shape[1]
    w_in = gathered_over_ctx(jnp.concatenate([w_query, w_key, value_weight], axis=1))

    own_normed = root_mean_scale(own_rows, pre_gain).astype(jnp.bfloat16)
    normed = lax.all_gather(own_normed, HEAD, axis=0, tiled=True)
    normed, w_output = lax.optimization_barrier((normed, w_output))
    out_weight = gathered_pair_first(w_output)
    tok_count = normed.shape[0]
    projected = jnp.dot(normed, w_in, preferred_element_type=jnp.float32)
    query_raw = projected[:, :q_cols]
    key_unnormed = projected[:, q_cols : q_cols + k_cols]
    value_unnormed = projected[:, q_cols + k_cols :]

    local_heads = q_cols // HEAD_SIZE
    local_groups = k_cols // HEAD_SIZE
    heads_per_group = local_heads // local_groups
    ctx_index = lax.axis_index(CTX)
    token_places = ctx_index * tok_count + jnp.arange(tok_count, dtype=jnp.int32)
    query_matrix = (
        apply_rotary(
            root_mean_scale(query_raw.reshape(tok_count, local_heads, HEAD_SIZE), query_gain),
            token_places,
        )
        * query_scale
    ).astype(jnp.bfloat16)
    projected_keys = apply_rotary(
        root_mean_scale(key_unnormed.reshape(tok_count, local_groups, HEAD_SIZE), key_norm_gain),
        token_places,
    ).astype(jnp.bfloat16)
    projected_values = value_unnormed.astype(jnp.bfloat16)
    key_value = jnp.stack(
        [projected_keys.reshape(tok_count, local_groups * HEAD_SIZE), projected_values]
    )
    pieces = [passed_along(key_value, CTX, 1)]
    extended = jnp.concatenate(pieces + [key_value], axis=1)
    band_keys = extended[0].reshape(-1, local_groups, HEAD_SIZE)
    band_values = extended[1].reshape(-1, local_groups, HEAD_SIZE)
    block_rows = min(512, tok_count)
    grouped_queries = query_matrix.reshape(tok_count, local_groups, heads_per_group, HEAD_SIZE)
    outputs = []
    for block_index in range(tok_count // block_rows):
        first_row = block_index * block_rows
        query_block = grouped_queries[first_row : first_row + block_rows]
        key_block = band_keys[first_row : first_row + block_rows + WINDOW_SPAN]
        value_block = band_values[first_row : first_row + block_rows + WINDOW_SPAN]
        scores = jnp.einsum(
            "qjgd,kjd->jgqk", query_block, key_block, preferred_element_type=jnp.float32
        )
        query_spots = token_places[first_row : first_row + block_rows]
        key_spots = (
            ctx_index * tok_count
            - WINDOW_SPAN
            + first_row
            + jnp.arange(block_rows + WINDOW_SPAN, dtype=jnp.int32)
        )
        allowed = (
            (key_spots[None, :] <= query_spots[:, None])
            & (key_spots[None, :] > query_spots[:, None] - WINDOW_SPAN)
            & (key_spots[None, :] >= 0)
        )
        scores = jnp.where(allowed, scores, mask_value)
        row_max = jnp.max(scores, axis=-1, keepdims=True)
        weights = jnp.exp(scores - row_max)
        row_sum = jnp.sum(weights, axis=-1, keepdims=True)
        probabilities = (weights / row_sum).astype(jnp.bfloat16)
        mixed = jnp.einsum(
            "jgqk,kjd->qjgd", probabilities, value_block, preferred_element_type=jnp.float32
        )
        outputs.append(mixed.astype(jnp.bfloat16).reshape(block_rows, local_heads * HEAD_SIZE))
    attended = jnp.concatenate(outputs, axis=0)

    partial_value = jnp.dot(attended, out_weight, preferred_element_type=jnp.float32).astype(
        jnp.bfloat16
    )
    summed = lax.psum_scatter(
        partial_value, HEAD, scatter_dimension=0, tiled=True
    ).astype(jnp.float32)
    result = own_rows + root_mean_scale(summed, post_gain)
    return result.astype(jnp.bfloat16)


def solution(mesh):
    ctx_size, head_size = mesh.devices.shape
    view = Mesh(
        mesh.devices.reshape(ctx_size // 2, 2, head_size // 2, 2), CTX + HEAD
    )
    rows_spec = P(CTX + HEAD, None)
    cols_spec = P(CTX, HEAD)
    return jax.shard_map(
        body,
        mesh=view,
        in_specs=(
            rows_spec,
            P(),
            cols_spec,
            cols_spec,
            cols_spec,
            P(),
            P(),
            P(HEAD + CTX, None),
            P(),
        ),
        out_specs=rows_spec,
        check_vma=False,
    )
```

```python
import jax
import jax.numpy as jnp
from jax import lax
from jax.sharding import Mesh, PartitionSpec as P

HEAD_SIZE = 128
WINDOW_SPAN = 1024


norm_eps = 1e-06
query_scale = 168.0 ** (-0.5)
rope_base = 10000.0
mask_value = -1e30
CTX = ("cx", "cy")
HEAD = ("hc", "core")


def passed_along(shard, axis, by):
    count = lax.axis_size(axis)
    pairs = [(i, i + by) for i in range(count) if 0 <= i + by < count]
    return lax.ppermute(shard, axis, pairs)


def rotated(shard, axis, by):
    count = lax.axis_size(axis)
    pairs = [(i, (i + by) % count) for i in range(count)]
    return lax.ppermute(shard, axis, pairs)


def placed(parts, me, count):
    stacked = jnp.zeros((count,) + parts[0].shape, parts[0].dtype)
    for i, part in enumerate(parts):
        stacked = lax.dynamic_update_index_in_dim(stacked, part, (me + i) % count, 0)
    return stacked


def ring_over_cx(piece):
    half = piece.shape[0] // 2
    from_left = rotated(piece, "cx", 1)
    from_right = rotated(piece, "cx", -1)
    far = jnp.concatenate(
        [rotated(from_left[:half], "cx", 1), rotated(from_right[half:], "cx", -1)]
    )
    return [piece, from_right, far, from_left]


def gathered_over_ctx(piece):
    cy = lax.axis_index("cy")
    cx = lax.axis_index("cx")
    own = ring_over_cx(piece)
    partner = ring_over_cx(rotated(piece, "cy", 1))
    pairs = [placed([a, b], cy, 2) for a, b in zip(own, partner)]
    ring = placed(pairs, cx, 4)
    return ring.reshape((8 * piece.shape[0],) + piece.shape[1:])


def gathered_with_partner(piece, crossed):
    cy = lax.axis_index("cy")
    cx = lax.axis_index("cx")
    own = ring_over_cx(piece)
    partner = ring_over_cx(crossed)
    pairs = [placed([a, b], cy, 2) for a, b in zip(own, partner)]
    ring = placed(pairs, cx, 4)
    return ring.reshape((8 * piece.shape[0],) + piece.shape[1:])


def root_mean_scale(values, scaling):
    mean_sq = jnp.mean(values * values, axis=-1, keepdims=True)
    return values * lax.rsqrt(mean_sq + norm_eps) * scaling


def apply_rotary(values, token_places):
    full_width = values.shape[-1]
    half_width = full_width // 2
    frequency = rope_base ** (-jnp.arange(half_width, dtype=jnp.float32) * 2.0 / full_width)
    angles = token_places.astype(jnp.float32)[:, None] * frequency[None, :]
    cosine = jnp.cos(angles)[:, None, :]
    sine_part = jnp.sin(angles)[:, None, :]
    lower_half = values[..., :half_width]
    upper_half = values[..., half_width:]
    return jnp.concatenate(
        [
            lower_half * cosine - upper_half * sine_part,
            upper_half * cosine + lower_half * sine_part,
        ],
        axis=-1,
    )


def body(
    hidden_in,
    pre_gain,
    w_query,
    w_key,
    value_weight,
    query_gain,
    key_norm_gain,
    w_output,
    post_gain,
):
    own_rows = hidden_in.astype(jnp.float32)
    q_cols = w_query.shape[1]
    k_cols = w_key.shape[1]
    w_in = gathered_over_ctx(jnp.concatenate([w_query, w_key, value_weight], axis=1))

    own_normed = root_mean_scale(own_rows, pre_gain).astype(jnp.bfloat16)
    normed = lax.all_gather(own_normed, HEAD, axis=0, tiled=True)
    crossed = rotated(w_output, "cy", 1)
    normed, w_output, crossed = lax.optimization_barrier((normed, w_output, crossed))
    out_weight = gathered_with_partner(w_output, crossed)
    tok_count = normed.shape[0]
    projected = jnp.dot(normed, w_in, preferred_element_type=jnp.float32)
    query_raw = projected[:, :q_cols]
    key_unnormed = projected[:, q_cols : q_cols + k_cols]
    value_unnormed = projected[:, q_cols + k_cols :]

    local_heads = q_cols // HEAD_SIZE
    local_groups = k_cols // HEAD_SIZE
    heads_per_group = local_heads // local_groups
    ctx_index = lax.axis_index(CTX)
    token_places = ctx_index * tok_count + jnp.arange(tok_count, dtype=jnp.int32)
    query_matrix = (
        apply_rotary(
            root_mean_scale(query_raw.reshape(tok_count, local_heads, HEAD_SIZE), query_gain),
            token_places,
        )
        * query_scale
    ).astype(jnp.bfloat16)
    projected_keys = apply_rotary(
        root_mean_scale(key_unnormed.reshape(tok_count, local_groups, HEAD_SIZE), key_norm_gain),
        token_places,
    ).astype(jnp.bfloat16)
    projected_values = value_unnormed.astype(jnp.bfloat16)
    key_value = jnp.stack(
        [projected_keys.reshape(tok_count, local_groups * HEAD_SIZE), projected_values]
    )
    pieces = [passed_along(key_value, CTX, 1)]
    extended = jnp.concatenate(pieces + [key_value], axis=1)
    band_keys = extended[0].reshape(-1, local_groups, HEAD_SIZE)
    band_values = extended[1].reshape(-1, local_groups, HEAD_SIZE)
    block_rows = min(512, tok_count)
    grouped_queries = query_matrix.reshape(tok_count, local_groups, heads_per_group, HEAD_SIZE)
    outputs = []
    for block_index in range(tok_count // block_rows):
        first_row = block_index * block_rows
        query_block = grouped_queries[first_row : first_row + block_rows]
        key_block = band_keys[first_row : first_row + block_rows + WINDOW_SPAN]
        value_block = band_values[first_row : first_row + block_rows + WINDOW_SPAN]
        scores = jnp.einsum(
            "qjgd,kjd->jgqk", query_block, key_block, preferred_element_type=jnp.float32
        )
        query_spots = token_places[first_row : first_row + block_rows]
        key_spots = (
            ctx_index * tok_count
            - WINDOW_SPAN
            + first_row
            + jnp.arange(block_rows + WINDOW_SPAN, dtype=jnp.int32)
        )
        allowed = (
            (key_spots[None, :] <= query_spots[:, None])
            & (key_spots[None, :] > query_spots[:, None] - WINDOW_SPAN)
            & (key_spots[None, :] >= 0)
        )
        scores = jnp.where(allowed, scores, mask_value)
        row_max = jnp.max(scores, axis=-1, keepdims=True)
        weights = jnp.exp(scores - row_max)
        row_sum = jnp.sum(weights, axis=-1, keepdims=True)
        probabilities = (weights / row_sum).astype(jnp.bfloat16)
        mixed = jnp.einsum(
            "jgqk,kjd->qjgd", probabilities, value_block, preferred_element_type=jnp.float32
        )
        outputs.append(mixed.astype(jnp.bfloat16).reshape(block_rows, local_heads * HEAD_SIZE))
    attended = jnp.concatenate(outputs, axis=0)

    partial_value = jnp.dot(attended, out_weight, preferred_element_type=jnp.float32).astype(
        jnp.bfloat16
    )
    summed = lax.psum_scatter(
        partial_value, HEAD, scatter_dimension=0, tiled=True
    ).astype(jnp.float32)
    result = own_rows + root_mean_scale(summed, post_gain)
    return result.astype(jnp.bfloat16)


def solution(mesh):
    ctx_size, head_size = mesh.devices.shape
    view = Mesh(
        mesh.devices.reshape(ctx_size // 2, 2, head_size // 2, 2), CTX + HEAD
    )
    rows_spec = P(CTX + HEAD, None)
    cols_spec = P(CTX, HEAD)
    return jax.shard_map(
        body,
        mesh=view,
        in_specs=(
            rows_spec,
            P(),
            cols_spec,
            cols_spec,
            cols_spec,
            P(),
            P(),
            P(HEAD + CTX, None),
            P(),
        ),
        out_specs=rows_spec,
        check_vma=False,
    )
```
